512 devices in a mesh: front: 8 (over z), grid: 16 (over y, x_hi), depth: 4 (over x_lo, core).
Axes of the slice: x: 4 (x_hi: 2, x_lo: 2; x = x_hi * 2 + x_lo), y: 8, z: 8, core: 2. Of those that a mesh axis runs over, the one named last changes fastest.
Arguments:
- panel_base: float32 [8, 1, 16, 256, 256], P('front', None, 'grid'), as said below
- slab_base: float32 [8, 1, 16, 256, 1024], P('front', None, 'grid', None, 'depth'), may hold values from -6 to 6
- child_tiles: float32 [8, 16, 4, 14, 256, 256], P('front', 'grid', 'depth'), may hold values from -3 to 3
- child_maps: int32 [8, 16, 4, 14, 2], P('front', 'grid', 'depth'), may hold values from 0 to 15, as said below
- front_orders: int32 [8], P('front'), may hold values from 1280 to 4096, as said below
Outputs:
- panel_factor: float32 [8, 1, 16, 256, 256], P('front', None, 'grid')
- schur: float32 [8, 1, 16, 256, 1024], P('front', None, 'grid', None, 'depth')
The draws below stay inside these ranges and needn't reach their ends.
Inputs may be any that keep to these rules, and one draw needn't show every extreme that they name: Rows r = 0, g = 0 of each front's panel_base form a symmetric positive definite tile. `child_maps`: entry 0 is a parent tile row, entry 1 a tile column from 0 to 4, never both 0. A tile's owner is its parent tile row modulo 16; among one device's 14 tiles at most 2 have the same owner, and in every front one owner receives exactly 2 tiles from every device. `front_orders`: A multiple of 256; in every draw some front has the order 4096.
All inputs are finite; a program needn't handle non-finite values.
Results may differ from the reference program's by a relative error of at most 0.0003.
Values sent between devices are 32-bit elements; how exact they have to be, the bound alone decides.
No kernel may reach another device: no remote copies, remote signals or barrier semaphores. Data moves between devices by JAX's collectives and lax.ppermute only.
A program may use at most 64 MiB of HBM per device.

```python
import jax
import jax.numpy as jnp
from jax import lax

TILE = 256
ORDER = 4096
NEXT = 4
CAP = 2
KIDS = 14
ROUNDS = 1
SLAB = 1024
FRONTS = 8
N_GRID = 16
N_DEPTH = 4


def draw_panel_base(key, part):
    key = jax.random.fold_in(key, 31)
    noise_key, diag_key = jax.random.split(key)
    shape = (FRONTS, ROUNDS, N_GRID, TILE, TILE)
    noise = jnp.clip(jax.random.normal(noise_key, shape, jnp.float32), -4.0, 4.0)
    corner = noise[:, 0, 0]
    symmetric = 0.5 * (corner + jnp.swapaxes(corner, -1, -2))
    diagonal = jax.random.uniform(diag_key, (FRONTS, TILE), jnp.float32, 2.0, 4.0) * TILE ** 0.5
    corner = symmetric + jnp.eye(TILE, dtype=jnp.float32)[None] * diagonal[:, None, :]
    return noise.at[:, 0, 0].set(corner)


def draw_child_maps(key, part):
    key = jax.random.fold_in(key, 57)
    star_key, score_key, round_key, column_key = jax.random.split(key, 4)
    shape = (FRONTS, N_GRID, N_DEPTH, KIDS)
    star = jax.random.randint(star_key, (FRONTS, 1, 1, 1), 0, N_GRID)
    scores = jax.random.randint(score_key, (FRONTS, N_GRID, N_DEPTH, N_GRID - 1), 0, 65536) * N_GRID + jnp.arange(N_GRID - 1)
    order_perm = jnp.argsort(scores, axis=-1, stable=True).astype(jnp.int32)
    others = (star + 1 + order_perm) % N_GRID
    pairs = jnp.concatenate([jnp.broadcast_to(star, (FRONTS, N_GRID, N_DEPTH, 1)), others[..., :KIDS // CAP - 1]], axis=-1)
    owners = jnp.repeat(pairs, CAP, axis=-1)
    rounds_drawn = jax.random.randint(round_key, shape, 0, ROUNDS)
    parent_row = owners + N_GRID * rounds_drawn
    parent_col = jax.random.randint(column_key, shape, 0, NEXT + 1)
    parent_col = jnp.where((parent_row == 0) & (parent_col == 0), 1, parent_col)
    return jnp.stack([parent_row, parent_col], axis=-1).astype(jnp.int32)


def draw_front_orders(key, part):
    key = jax.random.fold_in(key, 83)
    count_key, top_key = jax.random.split(key)
    counts = jax.random.randint(count_key, (FRONTS,), NEXT + 1, ORDER // TILE + 1)
    top = jax.random.randint(top_key, (), 0, FRONTS)
    counts = jnp.where(jnp.arange(FRONTS) == top, ORDER // TILE, counts)
    return (counts * TILE).astype(jnp.int32)


def steps_of(rng, extent, shards, low, top_value):
    gain = 1.0
    for position, parts in shards:
        draws = jax.random.uniform(jax.random.fold_in(jax.random.fold_in(rng, 6), position), (parts,), jnp.float32, low / len(shards), top_value / len(shards))
        gain = gain * jnp.repeat(jnp.exp(draws), extent[position] // parts).reshape((-1,) + (1,) * (len(extent) - 1 - position))
    return gain


def gaussian(own_key, dims, width, bound, cuts=(), kind=jnp.bfloat16):
    gain = steps_of(own_key, dims, cuts, -0.22, 0.18) if cuts else 1.0
    values = jax.random.normal(own_key, dims, jnp.float32) * width * gain
    return jnp.minimum(jnp.maximum(values, -bound), bound).astype(kind)


def setup_inputs(seed: int = 0) -> dict:
    key_list = jax.random.split(jax.random.key(seed), 6)
    return {
        "panel_base": draw_panel_base(jax.random.fold_in(key_list[5], 71), 0),
        "slab_base": gaussian(key_list[1], (FRONTS, ROUNDS, N_GRID, TILE, SLAB), 1.0, 6.0, ((0, 8), (2, 16), (4, 4)), jnp.float32),
        "child_tiles": gaussian(key_list[2], (FRONTS, N_GRID, N_DEPTH, KIDS, TILE, TILE), 0.5, 3.0, ((0, 8), (1, 16), (2, 4)), jnp.float32),
        "child_maps": draw_child_maps(jax.random.fold_in(key_list[5], 71), 0),
        "front_orders": draw_front_orders(jax.random.fold_in(key_list[5], 71), 0),
    }


def one_front(inputs):
    panel_tiles, slab_tiles, child_part, map_part, order_value = inputs
    tile_count = ORDER // TILE
    panel_flat = panel_tiles.reshape(tile_count, TILE, TILE)
    slab_flat = slab_tiles.reshape(tile_count, TILE, NEXT, TILE).transpose(0, 2, 1, 3)
    window = jnp.concatenate([panel_flat[:, None], slab_flat], axis=1)
    positions = (map_part[..., 0] * (NEXT + 1) + map_part[..., 1]).reshape(-1).astype(jnp.int32)
    added = jax.ops.segment_sum(child_part.reshape(-1, TILE, TILE), positions, num_segments=tile_count * (NEXT + 1))
    window = window + added.reshape(tile_count, NEXT + 1, TILE, TILE)
    live_rows = (jnp.arange(tile_count) * TILE < order_value).astype(jnp.float32)
    window = window * live_rows[:, None, None, None]
    corner_factor = jnp.linalg.cholesky(window[0, 0])
    solved = lax.linalg.triangular_solve(jnp.broadcast_to(corner_factor, (tile_count, TILE, TILE)), window[:, 0], left_side=False, lower=True, transpose_a=True)
    factored = jnp.concatenate([corner_factor[None], solved[1:]], axis=0)
    wanted = factored[1:NEXT + 1]
    update = jnp.einsum('tai,jbi->tjab', factored, wanted, precision=lax.Precision.HIGHEST)
    schur_block = window[:, 1:] - update
    schur_block = schur_block.transpose(0, 2, 1, 3).reshape(ROUNDS, N_GRID, TILE, SLAB)
    return (factored.reshape(ROUNDS, N_GRID, TILE, TILE), schur_block)

def reference(panel_base, slab_base, child_tiles, child_maps, front_orders):
    panel_factor, schur = lax.map(one_front, (panel_base, slab_base, child_tiles, child_maps, front_orders))
    return (panel_factor, schur)
```

```python
import jax
import jax.numpy as jnp
from jax import lax
from jax.experimental import pallas as pl
from jax.experimental.pallas import tpu as pltpu
from jax.sharding import PartitionSpec as P

CAP = 2
HIGH = lax.Precision.HIGHEST


def accumulate(place, arrived, positions):
    slots, tile, _ = arrived.shape

    def kernel(place_ref, x_ref, o_ref):
        o_ref[...] = jnp.zeros_like(o_ref)

        def body(s, carry):
            p = place_ref[s]
            o_ref[p] = o_ref[p] + x_ref[s]
            return carry

        lax.fori_loop(0, slots, body, 0)

    return pl.pallas_call(
        kernel,
        grid_spec=pltpu.PrefetchScalarGridSpec(
            num_scalar_prefetch=1,
            grid=(1,),
            in_specs=[pl.BlockSpec((slots, tile, tile), lambda i, p: (0, 0, 0))],
            out_specs=pl.BlockSpec((positions + 1, tile, tile), lambda i, p: (0, 0, 0)),
        ),
        out_shape=jax.ShapeDtypeStruct((positions + 1, tile, tile), jnp.float32),
    )(place, arrived)


def route(src, tiles, slots):
    kids, tile, _ = tiles.shape

    def kernel(src_ref, x_ref, o_ref):
        def body(s, carry):
            k = src_ref[s]
            valid = k < kids
            kk = jnp.minimum(k, kids - 1)
            o_ref[s] = jnp.where(valid, x_ref[kk], 0.0)
            return carry

        lax.fori_loop(0, slots, body, 0)

    return pl.pallas_call(
        kernel,
        grid_spec=pltpu.PrefetchScalarGridSpec(
            num_scalar_prefetch=1,
            grid=(1,),
            in_specs=[pl.BlockSpec((kids, tile, tile), lambda i, s: (0, 0, 0))],
            out_specs=pl.BlockSpec((slots, tile, tile), lambda i, s: (0, 0, 0)),
        ),
        out_shape=jax.ShapeDtypeStruct((slots, tile, tile), jnp.float32),
    )(src, tiles)


def on_device(panel_base, slab_base, child_tiles, child_maps, front_orders):
    grid_size = lax.axis_size("grid")
    depth_size = lax.axis_size("depth")
    grid_pos = lax.axis_index("grid")
    depth_pos = lax.axis_index("depth")
    rounds = panel_base.shape[1]
    tile = panel_base.shape[3]
    column_share = slab_base.shape[4] // tile
    next_tiles = column_share * depth_size
    positions = rounds * (next_tiles + 1)
    assert rounds == 1 and column_share == 1 and depth_size == 4
    assert panel_base.shape[0] == 1

    corner = panel_base[0, 0, 0]
    have = grid_pos == 0
    steps = []
    s = 1
    while s < grid_size:
        steps.append(s)
        s *= 2
    for s in reversed(steps):
        perm = [(i, i + s) for i in range(grid_size) if i % (2 * s) == 0 and i + s < grid_size]
        got = lax.ppermute(corner, "grid", perm)
        is_dst = (grid_pos % (2 * s)) == s
        corner = jnp.where(is_dst, got, corner)
    factor = jnp.linalg.cholesky(corner)
    eye = jnp.eye(tile, dtype=jnp.float32)
    inv_t = lax.linalg.triangular_solve(factor, eye, left_side=True, lower=True, transpose_a=True)

    tile_maps = child_maps[0, 0, 0]
    tile_data = child_tiles[0, 0, 0]
    kid_count = tile_data.shape[0]
    parent_row = tile_maps[:, 0]
    parent_col = tile_maps[:, 1]
    owners = parent_row % grid_size
    same_owner = owners[:, None] == owners[None, :]
    earlier = jnp.arange(kid_count)[None, :] < jnp.arange(kid_count)[:, None]
    bucket_slot = jnp.sum((same_owner & earlier).astype(jnp.int32), axis=1)
    destination = owners * CAP + bucket_slot
    slots = grid_size * CAP
    hit = destination[None, :] == jnp.arange(slots)[:, None]
    kid_ids = jnp.arange(kid_count, dtype=jnp.int32)
    src = jnp.sum(jnp.where(hit, kid_ids[None, :], 0), axis=1) + jnp.where(
        jnp.any(hit, axis=1), 0, kid_count
    )
    src = src.astype(jnp.int32)
    position = (parent_row // grid_size * (next_tiles + 1) + parent_col).astype(jnp.int32)
    send_place = jnp.sum(jnp.where(hit, position[None, :], 0), axis=1) + jnp.where(
        jnp.any(hit, axis=1), 0, positions
    )
    send_place = send_place.astype(jnp.int32)
    send_tiles = route(src, tile_data, slots).reshape(grid_size, CAP, tile, tile)
    arrived = lax.all_to_all(send_tiles, "grid", 0, 0, tiled=True)
    arrived_place = lax.all_to_all(send_place.reshape(grid_size, CAP), "grid", 0, 0, tiled=True)
    partial = accumulate(arrived_place.reshape(slots), arrived.reshape(slots, tile, tile), positions)

    panel_part = partial[0]
    slab_part = partial[1:positions]
    core_bit = depth_pos % 2
    chip_bit = depth_pos // 2
    other = 1 - core_bit
    send1 = jnp.stack([panel_part, slab_part[other], slab_part[other + 2]])
    keep1 = jnp.stack([panel_part, slab_part[core_bit], slab_part[core_bit + 2]])
    got1 = lax.ppermute(send1, "depth", [(0, 1), (1, 0), (2, 3), (3, 2)])
    sum1 = keep1 + got1
    send2 = jnp.stack([sum1[0], sum1[1 + (1 - chip_bit)]])
    got2 = lax.ppermute(send2, "depth", [(0, 2), (2, 0), (1, 3), (3, 1)])
    panel_sum = sum1[0] + got2[0]
    slab_sum = sum1[1 + chip_bit] + got2[1]

    live = (grid_pos * tile < front_orders[0]).astype(jnp.float32)
    front_panel = (panel_base[0, 0, 0] + panel_sum) * live
    front_slab = (slab_base[0, 0, 0] + slab_sum) * live

    solved = jnp.dot(front_panel, inv_t, precision=HIGH)
    factored = jnp.where(grid_pos == 0, factor, solved)

    wanted = factored
    for s in reversed(steps):
        perm = []
        for d in range(depth_size):
            for v in range(0, grid_size, 2 * s):
                if v + s < grid_size:
                    g_src = (v + d + 1) % grid_size
                    g_dst = (v + s + d + 1) % grid_size
                    perm.append((g_src * depth_size + d, g_dst * depth_size + d))
        got = lax.ppermute(wanted, ("grid", "depth"), perm)
        v_here = (grid_pos - depth_pos - 1) % grid_size
        is_dst = (v_here % (2 * s)) == s
        wanted = jnp.where(is_dst, got, wanted)

    update = lax.dot_general(
        factored, wanted, (((1,), (1,)), ((), ())), precision=HIGH
    )
    schur_block = front_slab - update
    return (factored[None, None, None], schur_block[None, None, None])


def solution(mesh):
    in_specs = (
        P("front", None, "grid", None, None),
        P("front", None, "grid", None, "depth"),
        P("front", "grid", "depth", None, None, None),
        P("front", "grid", "depth", None, None),
        P("front"),
    )
    out_specs = (P("front", None, "grid", None, None), P("front", None, "grid", None, "depth"))
    return jax.shard_map(
        on_device, mesh=mesh, in_specs=in_specs, out_specs=out_specs, check_vma=False
    )
```

```python
import jax
import jax.numpy as jnp
from jax import lax
from jax.experimental import pallas as pl
from jax.experimental.pallas import tpu as pltpu
from jax.sharding import PartitionSpec as P

CAP = 2
HIGH = lax.Precision.HIGHEST


def accumulate(place, arrived, positions):
    slots, tile, _ = arrived.shape

    def kernel(place_ref, x_ref, o_ref):
        o_ref[...] = jnp.zeros_like(o_ref)

        def body(s, carry):
            p = place_ref[s]
            o_ref[p] = o_ref[p] + x_ref[s]
            return carry

        lax.fori_loop(0, slots, body, 0)

    return pl.pallas_call(
        kernel,
        grid_spec=pltpu.PrefetchScalarGridSpec(
            num_scalar_prefetch=1,
            grid=(1,),
            in_specs=[pl.BlockSpec((slots, tile, tile), lambda i, p: (0, 0, 0))],
            out_specs=pl.BlockSpec((positions + 1, tile, tile), lambda i, p: (0, 0, 0)),
        ),
        out_shape=jax.ShapeDtypeStruct((positions + 1, tile, tile), jnp.float32),
    )(place, arrived)


def route(src, tiles, slots):
    kids, tile, _ = tiles.shape

    def kernel(src_ref, x_ref, o_ref):
        def body(s, carry):
            k = src_ref[s]
            valid = k < kids
            kk = jnp.minimum(k, kids - 1)
            o_ref[s] = jnp.where(valid, x_ref[kk], 0.0)
            return carry

        lax.fori_loop(0, slots, body, 0)

    return pl.pallas_call(
        kernel,
        grid_spec=pltpu.PrefetchScalarGridSpec(
            num_scalar_prefetch=1,
            grid=(1,),
            in_specs=[pl.BlockSpec((kids, tile, tile), lambda i, s: (0, 0, 0))],
            out_specs=pl.BlockSpec((slots, tile, tile), lambda i, s: (0, 0, 0)),
        ),
        out_shape=jax.ShapeDtypeStruct((slots, tile, tile), jnp.float32),
    )(src, tiles)


def on_device(panel_base, slab_base, child_tiles, child_maps, front_orders):
    grid_size = lax.axis_size("grid")
    depth_size = lax.axis_size("depth")
    grid_pos = lax.axis_index("grid")
    depth_pos = lax.axis_index("depth")
    rounds = panel_base.shape[1]
    tile = panel_base.shape[3]
    column_share = slab_base.shape[4] // tile
    next_tiles = column_share * depth_size
    positions = rounds * (next_tiles + 1)
    assert rounds == 1 and column_share == 1 and depth_size == 4
    assert panel_base.shape[0] == 1

    corner = panel_base[0, 0, 0]
    have = grid_pos == 0
    steps = []
    s = 1
    while s < grid_size:
        steps.append(s)
        s *= 2
    for s in reversed(steps):
        perm = [(i, i + s) for i in range(grid_size) if i % (2 * s) == 0 and i + s < grid_size]
        got = lax.ppermute(corner, "grid", perm)
        is_dst = (grid_pos % (2 * s)) == s
        corner = jnp.where(is_dst, got, corner)

    tile_maps = child_maps[0, 0, 0]
    tile_data = child_tiles[0, 0, 0]
    kid_count = tile_data.shape[0]
    parent_row = tile_maps[:, 0]
    parent_col = tile_maps[:, 1]
    owners = parent_row % grid_size
    same_owner = owners[:, None] == owners[None, :]
    earlier = jnp.arange(kid_count)[None, :] < jnp.arange(kid_count)[:, None]
    bucket_slot = jnp.sum((same_owner & earlier).astype(jnp.int32), axis=1)
    destination = owners * CAP + bucket_slot
    slots = grid_size * CAP
    hit = destination[None, :] == jnp.arange(slots)[:, None]
    kid_ids = jnp.arange(kid_count, dtype=jnp.int32)
    src = jnp.sum(jnp.where(hit, kid_ids[None, :], 0), axis=1) + jnp.where(
        jnp.any(hit, axis=1), 0, kid_count
    )
    src = src.astype(jnp.int32)
    position = (parent_row // grid_size * (next_tiles + 1) + parent_col).astype(jnp.int32)
    send_place = jnp.sum(jnp.where(hit, position[None, :], 0), axis=1) + jnp.where(
        jnp.any(hit, axis=1), 0, positions
    )
    send_place = send_place.astype(jnp.int32)
    send_tiles = route(src, tile_data, slots).reshape(grid_size, CAP, tile, tile)
    corner, send_tiles = lax.optimization_barrier((corner, send_tiles))
    factor = jnp.linalg.cholesky(corner)
    eye = jnp.eye(tile, dtype=jnp.float32)
    inv_t = lax.linalg.triangular_solve(factor, eye, left_side=True, lower=True, transpose_a=True)
    arrived = lax.all_to_all(send_tiles, "grid", 0, 0, tiled=True)
    arrived_place = lax.all_to_all(send_place.reshape(grid_size, CAP), "grid", 0, 0, tiled=True)
    inv_t, factor, arrived = lax.optimization_barrier((inv_t, factor, arrived))
    partial = accumulate(arrived_place.reshape(slots), arrived.reshape(slots, tile, tile), positions)

    panel_part = partial[0]
    slab_part = partial[1:positions]
    core_bit = depth_pos % 2
    chip_bit = depth_pos // 2
    other = 1 - core_bit
    send1 = jnp.stack([panel_part, slab_part[other], slab_part[other + 2]])
    keep1 = jnp.stack([panel_part, slab_part[core_bit], slab_part[core_bit + 2]])
    got1 = lax.ppermute(send1, "depth", [(0, 1), (1, 0), (2, 3), (3, 2)])
    sum1 = keep1 + got1
    send2 = jnp.stack([sum1[0], sum1[1 + (1 - chip_bit)]])
    got2 = lax.ppermute(send2, "depth", [(0, 2), (2, 0), (1, 3), (3, 1)])
    panel_sum = sum1[0] + got2[0]
    slab_sum = sum1[1 + chip_bit] + got2[1]

    live = (grid_pos * tile < front_orders[0]).astype(jnp.float32)
    front_panel = (panel_base[0, 0, 0] + panel_sum) * live
    front_slab = (slab_base[0, 0, 0] + slab_sum) * live

    solved = jnp.dot(front_panel, inv_t, precision=HIGH)
    factored = jnp.where(grid_pos == 0, factor, solved)

    k_here = (grid_pos - depth_pos - 1) % grid_size
    wanted = factored
    for k in range(1, grid_size):
        perm = [
            ((d + 1) % grid_size * depth_size + d, (d + 1 + k) % grid_size * depth_size + d)
            for d in range(depth_size)
        ]
        got = lax.ppermute(factored, ("grid", "depth"), perm)
        wanted = jnp.where(k_here == k, got, wanted)

    update = lax.dot_general(
        factored, wanted, (((1,), (1,)), ((), ())), precision=HIGH
    )
    schur_block = front_slab - update
    return (factored[None, None, None], schur_block[None, None, None])


def solution(mesh):
    in_specs = (
        P("front", None, "grid", None, None),
        P("front", None, "grid", None, "depth"),
        P("front", "grid", "depth", None, None, None),
        P("front", "grid", "depth", None, None),
        P("front"),
    )
    out_specs = (P("front", None, "grid", None, None), P("front", None, "grid", None, "depth"))
    return jax.shard_map(
        on_device, mesh=mesh, in_specs=in_specs, out_specs=out_specs, check_vma=False
    )
```

```python
import jax
import jax.numpy as jnp
from jax import lax
from jax.experimental import pallas as pl
from jax.experimental.pallas import tpu as pltpu
from jax.sharding import PartitionSpec as P

CAP = 2
HIGH = lax.Precision.HIGHEST


def accumulate(place, arrived, positions):
    slots, rows, tile = arrived.shape

    def kernel(place_ref, x_ref, o_ref):
        o_ref[...] = jnp.zeros_like(o_ref)

        def body(s, carry):
            p = place_ref[s]
            o_ref[p] = o_ref[p] + x_ref[s, pl.ds(0, tile), :]
            return carry

        lax.fori_loop(0, slots, body, 0)

    return pl.pallas_call(
        kernel,
        grid_spec=pltpu.PrefetchScalarGridSpec(
            num_scalar_prefetch=1,
            grid=(1,),
            in_specs=[pl.BlockSpec((slots, rows, tile), lambda i, p: (0, 0, 0))],
            out_specs=pl.BlockSpec((positions + 1, tile, tile), lambda i, p: (0, 0, 0)),
        ),
        out_shape=jax.ShapeDtypeStruct((positions + 1, tile, tile), jnp.float32),
    )(place, arrived)


def route(src, place, tiles, slots):
    kids, tile, _ = tiles.shape

    def kernel(src_ref, place_ref, x_ref, o_ref):
        def body(s, carry):
            k = src_ref[s]
            valid = k < kids
            kk = jnp.minimum(k, kids - 1)
            o_ref[s, pl.ds(0, tile), :] = jnp.where(valid, x_ref[kk], 0.0)
            o_ref[s, pl.ds(tile, 8), :] = jnp.full((8, tile), place_ref[s], jnp.int32).astype(
                jnp.float32
            )
            return carry

        lax.fori_loop(0, slots, body, 0)

    return pl.pallas_call(
        kernel,
        grid_spec=pltpu.PrefetchScalarGridSpec(
            num_scalar_prefetch=2,
            grid=(1,),
            in_specs=[pl.BlockSpec((kids, tile, tile), lambda i, s, p: (0, 0, 0))],
            out_specs=pl.BlockSpec((slots, tile + 8, tile), lambda i, s, p: (0, 0, 0)),
        ),
        out_shape=jax.ShapeDtypeStruct((slots, tile + 8, tile), jnp.float32),
    )(src, place, tiles)


def fan_out(x, hop, v_here, n, index_of, axes, groups):
    out = x
    for m in range(1, 4):
        perm = []
        for d in range(groups):
            for v in range(0, n, 4 * hop):
                if v + m * hop < n:
                    perm.append((index_of(v, d), index_of(v + m * hop, d)))
        got = lax.ppermute(x, axes, perm)
        out = jnp.where(v_here % (4 * hop) == m * hop, got, out)
    return out


def on_device(panel_base, slab_base, child_tiles, child_maps, front_orders):
    grid_size = lax.axis_size("grid")
    depth_size = lax.axis_size("depth")
    grid_pos = lax.axis_index("grid")
    depth_pos = lax.axis_index("depth")
    rounds = panel_base.shape[1]
    tile = panel_base.shape[3]
    column_share = slab_base.shape[4] // tile
    next_tiles = column_share * depth_size
    positions = rounds * (next_tiles + 1)
    assert rounds == 1 and column_share == 1 and depth_size == 4
    assert panel_base.shape[0] == 1 and grid_size == 16
    fan_steps = (grid_size // 4, 1)

    tile_maps = child_maps[0, 0, 0]
    tile_data = child_tiles[0, 0, 0]
    kid_count = tile_data.shape[0]
    parent_row = tile_maps[:, 0]
    parent_col = tile_maps[:, 1]
    owners = parent_row % grid_size
    same_owner = owners[:, None] == owners[None, :]
    earlier = jnp.arange(kid_count)[None, :] < jnp.arange(kid_count)[:, None]
    bucket_slot = jnp.sum((same_owner & earlier).astype(jnp.int32), axis=1)
    destination = owners * CAP + bucket_slot
    slots = grid_size * CAP
    hit = destination[None, :] == jnp.arange(slots)[:, None]
    kid_ids = jnp.arange(kid_count, dtype=jnp.int32)
    src = jnp.sum(jnp.where(hit, kid_ids[None, :], 0), axis=1) + jnp.where(
        jnp.any(hit, axis=1), 0, kid_count
    )
    src = src.astype(jnp.int32)
    position = (parent_row // grid_size * (next_tiles + 1) + parent_col).astype(jnp.int32)
    send_place = jnp.sum(jnp.where(hit, position[None, :], 0), axis=1) + jnp.where(
        jnp.any(hit, axis=1), 0, positions
    )
    send_place = send_place.astype(jnp.int32)
    send_tiles = route(src, send_place, tile_data, slots).reshape(grid_size, CAP, tile + 8, tile)

    corner = panel_base[0, 0, 0]
    for level, hop in enumerate(fan_steps):
        if level == 1:
            corner, send_tiles = lax.optimization_barrier((corner, send_tiles))
        corner = fan_out(corner, hop, grid_pos, grid_size, lambda v, d: v, "grid", 1)
    corner, send_tiles = lax.optimization_barrier((corner, send_tiles))
    factor = jnp.linalg.cholesky(corner)
    eye = jnp.eye(tile, dtype=jnp.float32)
    inv_t = lax.linalg.triangular_solve(factor, eye, left_side=True, lower=True, transpose_a=True)
    arrived = lax.all_to_all(send_tiles, "grid", 0, 0, tiled=True)
    arrived_place = arrived[:, :, tile, 0].astype(jnp.int32)
    inv_t, factor, arrived = lax.optimization_barrier((inv_t, factor, arrived))
    partial = accumulate(arrived_place.reshape(slots), arrived.reshape(slots, tile + 8, tile), positions)

    panel_part = partial[0]
    slab_part = partial[1:positions]
    core_bit = depth_pos % 2
    chip_bit = depth_pos // 2
    other = 1 - core_bit
    send1 = jnp.stack([panel_part, slab_part[other], slab_part[other + 2]])
    keep1 = jnp.stack([panel_part, slab_part[core_bit], slab_part[core_bit + 2]])
    got1 = lax.ppermute(send1, "depth", [(0, 1), (1, 0), (2, 3), (3, 2)])
    sum1 = keep1 + got1
    send2 = jnp.stack([sum1[0], sum1[1 + (1 - chip_bit)]])
    got2 = lax.ppermute(send2, "depth", [(0, 2), (2, 0), (1, 3), (3, 1)])
    panel_sum = sum1[0] + got2[0]
    slab_sum = sum1[1 + chip_bit] + got2[1]

    live = (grid_pos * tile < front_orders[0]).astype(jnp.float32)
    front_panel = (panel_base[0, 0, 0] + panel_sum) * live
    front_slab = (slab_base[0, 0, 0] + slab_sum) * live

    solved = jnp.dot(front_panel, inv_t, precision=HIGH)
    factored = jnp.where(grid_pos == 0, factor, solved)

    v_here = (grid_pos - depth_pos - 1) % grid_size
    wanted = factored
    for hop in fan_steps:
        wanted = fan_out(
            wanted, hop, v_here, grid_size,
            lambda v, d: ((v + d + 1) % grid_size) * depth_size + d, ("grid", "depth"), depth_size,
        )

    update = lax.dot_general(
        factored, wanted, (((1,), (1,)), ((), ())), precision=HIGH
    )
    schur_block = front_slab - update
    return (factored[None, None, None], schur_block[None, None, None])


def solution(mesh):
    in_specs = (
        P("front", None, "grid", None, None),
        P("front", None, "grid", None, "depth"),
        P("front", "grid", "depth", None, None, None),
        P("front", "grid", "depth", None, None),
        P("front"),
    )
    out_specs = (P("front", None, "grid", None, None), P("front", None, "grid", None, "depth"))
    return jax.shard_map(
        on_device, mesh=mesh, in_specs=in_specs, out_specs=out_specs, check_vma=False
    )
```

```python
import jax
import jax.numpy as jnp
from jax import lax
from jax.experimental import pallas as pl
from jax.experimental.pallas import tpu as pltpu
from jax.sharding import PartitionSpec as P

CAP = 2
HIGH = lax.Precision.HIGHEST


def accumulate(place, arrived, positions):
    slots, rows, tile = arrived.shape

    def kernel(place_ref, x_ref, o_ref):
        o_ref[...] = jnp.zeros_like(o_ref)

        def body(s, carry):
            p = place_ref[s]
            o_ref[p] = o_ref[p] + x_ref[s, pl.ds(0, tile), :]
            return carry

        lax.fori_loop(0, slots, body, 0)

    return pl.pallas_call(
        kernel,
        grid_spec=pltpu.PrefetchScalarGridSpec(
            num_scalar_prefetch=1,
            grid=(1,),
            in_specs=[pl.BlockSpec((slots, rows, tile), lambda i, p: (0, 0, 0))],
            out_specs=pl.BlockSpec((positions + 1, tile, tile), lambda i, p: (0, 0, 0)),
        ),
        out_shape=jax.ShapeDtypeStruct((positions + 1, tile, tile), jnp.float32),
    )(place, arrived)


def route(src, place, tiles, slots):
    kids, tile, _ = tiles.shape

    def kernel(src_ref, place_ref, x_ref, o_ref):
        def body(s, carry):
            k = src_ref[s]
            valid = k < kids
            kk = jnp.minimum(k, kids - 1)
            o_ref[s, pl.ds(0, tile), :] = jnp.where(valid, x_ref[kk], 0.0)
            o_ref[s, pl.ds(tile, 8), :] = jnp.full((8, tile), place_ref[s], jnp.int32).astype(
                jnp.float32
            )
            return carry

        lax.fori_loop(0, slots, body, 0)

    return pl.pallas_call(
        kernel,
        grid_spec=pltpu.PrefetchScalarGridSpec(
            num_scalar_prefetch=2,
            grid=(1,),
            in_specs=[pl.BlockSpec((kids, tile, tile), lambda i, s, p: (0, 0, 0))],
            out_specs=pl.BlockSpec((slots, tile + 8, tile), lambda i, s, p: (0, 0, 0)),
        ),
        out_shape=jax.ShapeDtypeStruct((slots, tile + 8, tile), jnp.float32),
    )(src, place, tiles)


def fan_out(x, hop, v_here, n, index_of, axes, groups):
    out = x
    for m in range(1, 4):
        perm = []
        for d in range(groups):
            for v in range(0, n, 4 * hop):
                if v + m * hop < n:
                    perm.append((index_of(v, d), index_of(v + m * hop, d)))
        got = lax.ppermute(x, axes, perm)
        out = jnp.where(v_here % (4 * hop) == m * hop, got, out)
    return out


def on_device(panel_base, slab_base, child_tiles, child_maps, front_orders):
    grid_size = lax.axis_size("grid")
    depth_size = lax.axis_size("depth")
    grid_pos = lax.axis_index("grid")
    depth_pos = lax.axis_index("depth")
    rounds = panel_base.shape[1]
    tile = panel_base.shape[3]
    column_share = slab_base.shape[4] // tile
    next_tiles = column_share * depth_size
    positions = rounds * (next_tiles + 1)
    assert rounds == 1 and column_share == 1 and depth_size == 4
    assert panel_base.shape[0] == 1 and grid_size == 16
    fan_steps = (grid_size // 4, 1)

    tile_maps = child_maps[0, 0, 0]
    tile_data = child_tiles[0, 0, 0]
    kid_count = tile_data.shape[0]
    parent_row = tile_maps[:, 0]
    parent_col = tile_maps[:, 1]
    owners = parent_row % grid_size
    same_owner = owners[:, None] == owners[None, :]
    earlier = jnp.arange(kid_count)[None, :] < jnp.arange(kid_count)[:, None]
    bucket_slot = jnp.sum((same_owner & earlier).astype(jnp.int32), axis=1)
    destination = owners * CAP + bucket_slot
    slots = grid_size * CAP
    hit = destination[None, :] == jnp.arange(slots)[:, None]
    kid_ids = jnp.arange(kid_count, dtype=jnp.int32)
    src = jnp.sum(jnp.where(hit, kid_ids[None, :], 0), axis=1) + jnp.where(
        jnp.any(hit, axis=1), 0, kid_count
    )
    src = src.astype(jnp.int32)
    position = (parent_row // grid_size * (next_tiles + 1) + parent_col).astype(jnp.int32)
    send_place = jnp.sum(jnp.where(hit, position[None, :], 0), axis=1) + jnp.where(
        jnp.any(hit, axis=1), 0, positions
    )
    send_place = send_place.astype(jnp.int32)
    send_tiles = route(src, send_place, tile_data, slots).reshape(grid_size, CAP, tile + 8, tile)

    factor = jnp.linalg.cholesky(panel_base[0, 0, 0])
    eye = jnp.eye(tile, dtype=jnp.float32)
    inv_t = lax.linalg.triangular_solve(factor, eye, left_side=True, lower=True, transpose_a=True)
    arrived = lax.all_to_all(send_tiles, "grid", 0, 0, tiled=True)
    arrived_place = arrived[:, :, tile, 0].astype(jnp.int32)
    inv_t, factor, arrived = lax.optimization_barrier((inv_t, factor, arrived))
    for hop in fan_steps:
        inv_t = fan_out(inv_t, hop, grid_pos, grid_size, lambda v, d: v, "grid", 1)
    partial = accumulate(arrived_place.reshape(slots), arrived.reshape(slots, tile + 8, tile), positions)

    panel_part = partial[0]
    slab_part = partial[1:positions]
    core_bit = depth_pos % 2
    chip_bit = depth_pos // 2
    other = 1 - core_bit
    send1 = jnp.stack([panel_part, slab_part[other], slab_part[other + 2]])
    keep1 = jnp.stack([panel_part, slab_part[core_bit], slab_part[core_bit + 2]])
    got1 = lax.ppermute(send1, "depth", [(0, 1), (1, 0), (2, 3), (3, 2)])
    sum1 = keep1 + got1
    send2 = jnp.stack([sum1[0], sum1[1 + (1 - chip_bit)]])
    got2 = lax.ppermute(send2, "depth", [(0, 2), (2, 0), (1, 3), (3, 1)])
    panel_sum = sum1[0] + got2[0]
    slab_sum = sum1[1 + chip_bit] + got2[1]

    live = (grid_pos * tile < front_orders[0]).astype(jnp.float32)
    front_panel = (panel_base[0, 0, 0] + panel_sum) * live
    front_slab = (slab_base[0, 0, 0] + slab_sum) * live

    solved = jnp.dot(front_panel, inv_t, precision=HIGH)
    factored = jnp.where(grid_pos == 0, factor, solved)

    v_here = (grid_pos - depth_pos - 1) % grid_size
    wanted = factored
    for hop in fan_steps:
        wanted = fan_out(
            wanted, hop, v_here, grid_size,
            lambda v, d: ((v + d + 1) % grid_size) * depth_size + d, ("grid", "depth"), depth_size,
        )

    update = lax.dot_general(
        factored, wanted, (((1,), (1,)), ((), ())), precision=HIGH
    )
    schur_block = front_slab - update
    return (factored[None, None, None], schur_block[None, None, None])


def solution(mesh):
    in_specs = (
        P("front", None, "grid", None, None),
        P("front", None, "grid", None, "depth"),
        P("front", "grid", "depth", None, None, None),
        P("front", "grid", "depth", None, None),
        P("front"),
    )
    out_specs = (P("front", None, "grid", None, None), P("front", None, "grid", None, "depth"))
    return jax.shard_map(
        on_device, mesh=mesh, in_specs=in_specs, out_specs=out_specs, check_vma=False
    )
```

```python
import jax
import jax.numpy as jnp
from jax import lax
from jax.experimental import pallas as pl
from jax.experimental.pallas import tpu as pltpu
from jax.sharding import PartitionSpec as P

CAP = 2
HIGH = lax.Precision.HIGHEST


def accumulate(place, keep_of, send_of, arrived, chunk):
    slots, rows, tile = arrived.shape

    def kernel(place_ref, keep_ref, send_ref, x_ref, k_out, s_out):
        @pl.when(pl.program_id(0) == 0)
        def _():
            k_out[...] = jnp.zeros_like(k_out)
            s_out[...] = jnp.zeros_like(s_out)

        base = pl.program_id(0) * chunk

        def body(i, carry):
            p = place_ref[base + i]
            x = x_ref[i, pl.ds(0, tile), :]
            k = keep_ref[p]
            kk = jnp.minimum(k, 2)
            k_out[kk] = k_out[kk] + jnp.where(k < 3, x, 0.0)
            j = send_ref[p]
            jj = jnp.minimum(j, 2)
            s_out[jj] = s_out[jj] + jnp.where(j < 3, x, 0.0)
            return carry

        lax.fori_loop(0, chunk, body, 0)

    out = jax.ShapeDtypeStruct((3, tile, tile), jnp.float32)
    return pl.pallas_call(
        kernel,
        grid_spec=pltpu.PrefetchScalarGridSpec(
            num_scalar_prefetch=3,
            grid=(slots // chunk,),
            in_specs=[pl.BlockSpec((chunk, rows, tile), lambda i, a, b, c: (i, 0, 0))],
            out_specs=[
                pl.BlockSpec((3, tile, tile), lambda i, a, b, c: (0, 0, 0)),
                pl.BlockSpec((3, tile, tile), lambda i, a, b, c: (0, 0, 0)),
            ],
        ),
        out_shape=(out, out),
    )(place, keep_of, send_of, arrived)


def route(src, place, tiles, slots):
    kids, tile, _ = tiles.shape

    def kernel(src_ref, place_ref, x_ref, o_ref):
        def body(s, carry):
            k = src_ref[s]
            valid = k < kids
            kk = jnp.minimum(k, kids - 1)
            o_ref[s, pl.ds(0, tile), :] = jnp.where(valid, x_ref[kk], 0.0)
            o_ref[s, pl.ds(tile, 8), :] = jnp.full((8, tile), place_ref[s], jnp.int32).astype(
                jnp.float32
            )
            return carry

        lax.fori_loop(0, slots, body, 0)

    return pl.pallas_call(
        kernel,
        grid_spec=pltpu.PrefetchScalarGridSpec(
            num_scalar_prefetch=2,
            grid=(1,),
            in_specs=[pl.BlockSpec((kids, tile, tile), lambda i, s, p: (0, 0, 0))],
            out_specs=pl.BlockSpec((slots, tile + 8, tile), lambda i, s, p: (0, 0, 0)),
        ),
        out_shape=jax.ShapeDtypeStruct((slots, tile + 8, tile), jnp.float32),
    )(src, place, tiles)


def fan_out(x, hop, v_here, n, index_of, axes, groups):
    out = x
    for m in range(1, 4):
        perm = []
        for d in range(groups):
            for v in range(0, n, 4 * hop):
                if v + m * hop < n:
                    perm.append((index_of(v, d), index_of(v + m * hop, d)))
        got = lax.ppermute(x, axes, perm)
        out = jnp.where(v_here % (4 * hop) == m * hop, got, out)
    return out


def on_device(panel_base, slab_base, child_tiles, child_maps, front_orders):
    grid_size = lax.axis_size("grid")
    depth_size = lax.axis_size("depth")
    grid_pos = lax.axis_index("grid")
    depth_pos = lax.axis_index("depth")
    rounds = panel_base.shape[1]
    tile = panel_base.shape[3]
    column_share = slab_base.shape[4] // tile
    next_tiles = column_share * depth_size
    positions = rounds * (next_tiles + 1)
    assert rounds == 1 and column_share == 1 and depth_size == 4
    assert panel_base.shape[0] == 1 and grid_size == 16
    fan_steps = (grid_size // 4, 1)

    tile_maps = child_maps[0, 0, 0]
    tile_data = child_tiles[0, 0, 0]
    kid_count = tile_data.shape[0]
    parent_row = tile_maps[:, 0]
    parent_col = tile_maps[:, 1]
    owners = parent_row % grid_size
    same_owner = owners[:, None] == owners[None, :]
    earlier = jnp.arange(kid_count)[None, :] < jnp.arange(kid_count)[:, None]
    bucket_slot = jnp.sum((same_owner & earlier).astype(jnp.int32), axis=1)
    destination = owners * CAP + bucket_slot
    slots = grid_size * CAP
    hit = destination[None, :] == jnp.arange(slots)[:, None]
    kid_ids = jnp.arange(kid_count, dtype=jnp.int32)
    src = jnp.sum(jnp.where(hit, kid_ids[None, :], 0), axis=1) + jnp.where(
        jnp.any(hit, axis=1), 0, kid_count
    )
    src = src.astype(jnp.int32)
    position = (parent_row // grid_size * (next_tiles + 1) + parent_col).astype(jnp.int32)
    send_place = jnp.sum(jnp.where(hit, position[None, :], 0), axis=1) + jnp.where(
        jnp.any(hit, axis=1), 0, positions
    )
    send_place = send_place.astype(jnp.int32)
    send_tiles = route(src, send_place, tile_data, slots).reshape(grid_size, CAP, tile + 8, tile)

    factor = jnp.linalg.cholesky(panel_base[0, 0, 0])
    eye = jnp.eye(tile, dtype=jnp.float32)
    inv_t = lax.linalg.triangular_solve(factor, eye, left_side=True, lower=True, transpose_a=True)
    arrived = lax.all_to_all(send_tiles, "grid", 0, 0, tiled=True)
    arrived_place = arrived[:, :, tile, 0].astype(jnp.int32)
    inv_t, factor, arrived = lax.optimization_barrier((inv_t, factor, arrived))
    for hop in fan_steps:
        inv_t = fan_out(inv_t, hop, grid_pos, grid_size, lambda v, d: v, "grid", 1)
    core_bit = depth_pos % 2
    chip_bit = depth_pos // 2
    cols = jnp.arange(positions - 1, dtype=jnp.int32)
    col_keep = jnp.where(cols % 2 == core_bit, 1 + cols // 2, 3)
    col_send = jnp.where(cols % 2 != core_bit, 1 + cols // 2, 3)
    three = jnp.full((1,), 3, jnp.int32)
    zero = jnp.zeros((1,), jnp.int32)
    keep_of = jnp.concatenate([zero, col_keep, three]).astype(jnp.int32)
    send_of = jnp.concatenate([zero, col_send, three]).astype(jnp.int32)
    keep1, send1 = accumulate(
        arrived_place.reshape(slots), keep_of, send_of, arrived.reshape(slots, tile + 8, tile), 8
    )
    got1 = lax.ppermute(send1, "depth", [(0, 1), (1, 0), (2, 3), (3, 2)])
    sum1 = keep1 + got1
    send2 = jnp.stack([sum1[0], sum1[1 + (1 - chip_bit)]])
    got2 = lax.ppermute(send2, "depth", [(0, 2), (2, 0), (1, 3), (3, 1)])
    panel_sum = sum1[0] + got2[0]
    slab_sum = sum1[1 + chip_bit] + got2[1]

    live = (grid_pos * tile < front_orders[0]).astype(jnp.float32)
    front_panel = (panel_base[0, 0, 0] + panel_sum) * live
    front_slab = (slab_base[0, 0, 0] + slab_sum) * live

    v_here = (grid_pos - depth_pos - 1) % grid_size
    wanted = front_panel
    for hop in fan_steps:
        wanted = fan_out(
            wanted, hop, v_here, grid_size,
            lambda v, d: ((v + d + 1) % grid_size) * depth_size + d, ("grid", "depth"), depth_size,
        )
    solved = jnp.dot(front_panel, inv_t, precision=HIGH)
    factored = jnp.where(grid_pos == 0, factor, solved)
    wanted = jnp.dot(wanted, inv_t, precision=HIGH)

    update = lax.dot_general(
        factored, wanted, (((1,), (1,)), ((), ())), precision=HIGH
    )
    schur_block = front_slab - update
    return (factored[None, None, None], schur_block[None, None, None])


def solution(mesh):
    in_specs = (
        P("front", None, "grid", None, None),
        P("front", None, "grid", None, "depth"),
        P("front", "grid", "depth", None, None, None),
        P("front", "grid", "depth", None, None),
        P("front"),
    )
    out_specs = (P("front", None, "grid", None, None), P("front", None, "grid", None, "depth"))
    return jax.shard_map(
        on_device, mesh=mesh, in_specs=in_specs, out_specs=out_specs, check_vma=False
    )
```

```python
import jax
import jax.numpy as jnp
from jax import lax
from jax.experimental import pallas as pl
from jax.experimental.pallas import tpu as pltpu
from jax.sharding import PartitionSpec as P

CAP = 2
HIGH = lax.Precision.HIGHEST


def accumulate(place, keep_of, send_of, arrived, chunk):
    slots, rows, tile = arrived.shape

    def kernel(place_ref, keep_ref, send_ref, x_ref, k_out, s_out):
        @pl.when(pl.program_id(0) == 0)
        def _():
            k_out[...] = jnp.zeros_like(k_out)
            s_out[...] = jnp.zeros_like(s_out)

        base = pl.program_id(0) * chunk

        def body(i, carry):
            p = place_ref[base + i]
            x = x_ref[i, pl.ds(0, tile), :]
            k = keep_ref[p]
            kk = jnp.minimum(k, 2)
            k_out[kk] = k_out[kk] + jnp.where(k < 3, x, 0.0)
            j = send_ref[p]
            jj = jnp.minimum(j, 2)
            s_out[jj] = s_out[jj] + jnp.where(j < 3, x, 0.0)
            return carry

        lax.fori_loop(0, chunk, body, 0)

    out = jax.ShapeDtypeStruct((3, tile, tile), jnp.float32)
    return pl.pallas_call(
        kernel,
        grid_spec=pltpu.PrefetchScalarGridSpec(
            num_scalar_prefetch=3,
            grid=(slots // chunk,),
            in_specs=[pl.BlockSpec((chunk, rows, tile), lambda i, a, b, c: (i, 0, 0))],
            out_specs=[
                pl.BlockSpec((3, tile, tile), lambda i, a, b, c: (0, 0, 0)),
                pl.BlockSpec((3, tile, tile), lambda i, a, b, c: (0, 0, 0)),
            ],
        ),
        out_shape=(out, out),
    )(place, keep_of, send_of, arrived)


def route(src, place, tiles, slots):
    kids, tile, _ = tiles.shape

    def kernel(src_ref, place_ref, x_ref, o_ref):
        def body(s, carry):
            k = src_ref[s]
            valid = k < kids
            kk = jnp.minimum(k, kids - 1)
            o_ref[s, pl.ds(0, tile), :] = jnp.where(valid, x_ref[kk], 0.0)
            o_ref[s, pl.ds(tile, 8), :] = jnp.full((8, tile), place_ref[s], jnp.int32).astype(
                jnp.float32
            )
            return carry

        lax.fori_loop(0, slots, body, 0)

    return pl.pallas_call(
        kernel,
        grid_spec=pltpu.PrefetchScalarGridSpec(
            num_scalar_prefetch=2,
            grid=(1,),
            in_specs=[pl.BlockSpec((kids, tile, tile), lambda i, s, p: (0, 0, 0))],
            out_specs=pl.BlockSpec((slots, tile + 8, tile), lambda i, s, p: (0, 0, 0)),
        ),
        out_shape=jax.ShapeDtypeStruct((slots, tile + 8, tile), jnp.float32),
    )(src, place, tiles)


def fan_out(x, hop, v_here, n, index_of, axes, groups):
    out = x
    for m in range(1, 4):
        perm = []
        for d in range(groups):
            for v in range(0, n, 4 * hop):
                if v + m * hop < n:
                    perm.append((index_of(v, d), index_of(v + m * hop, d)))
        got = lax.ppermute(x, axes, perm)
        out = jnp.where(v_here % (4 * hop) == m * hop, got, out)
    return out


def on_device(panel_base, slab_base, child_tiles, child_maps, front_orders):
    grid_size = lax.axis_size("grid")
    depth_size = lax.axis_size("depth")
    grid_pos = lax.axis_index("grid")
    depth_pos = lax.axis_index("depth")
    rounds = panel_base.shape[1]
    tile = panel_base.shape[3]
    column_share = slab_base.shape[4] // tile
    next_tiles = column_share * depth_size
    positions = rounds * (next_tiles + 1)
    assert rounds == 1 and column_share == 1 and depth_size == 4
    assert panel_base.shape[0] == 1 and grid_size == 16
    fan_steps = (grid_size // 4, 1)
    assert grid_size % 4 == 0

    tile_maps = child_maps[0, 0, 0]
    tile_data = child_tiles[0, 0, 0]
    kid_count = tile_data.shape[0]
    parent_row = tile_maps[:, 0]
    parent_col = tile_maps[:, 1]
    owners = parent_row % grid_size
    same_owner = owners[:, None] == owners[None, :]
    earlier = jnp.arange(kid_count)[None, :] < jnp.arange(kid_count)[:, None]
    bucket_slot = jnp.sum((same_owner & earlier).astype(jnp.int32), axis=1)
    destination = owners * CAP + bucket_slot
    slots = grid_size * CAP
    hit = destination[None, :] == jnp.arange(slots)[:, None]
    kid_ids = jnp.arange(kid_count, dtype=jnp.int32)
    src = jnp.sum(jnp.where(hit, kid_ids[None, :], 0), axis=1) + jnp.where(
        jnp.any(hit, axis=1), 0, kid_count
    )
    src = src.astype(jnp.int32)
    position = (parent_row // grid_size * (next_tiles + 1) + parent_col).astype(jnp.int32)
    send_place = jnp.sum(jnp.where(hit, position[None, :], 0), axis=1) + jnp.where(
        jnp.any(hit, axis=1), 0, positions
    )
    send_place = send_place.astype(jnp.int32)
    send_tiles = route(src, send_place, tile_data, slots).reshape(grid_size, CAP, tile + 8, tile)

    factor = jnp.linalg.cholesky(panel_base[0, 0, 0])
    eye = jnp.eye(tile, dtype=jnp.float32)
    inv_t = lax.linalg.triangular_solve(factor, eye, left_side=True, lower=True, transpose_a=True)
    arrived = lax.all_to_all(send_tiles, "grid", 0, 0, tiled=True)
    arrived_place = arrived[:, :, tile, 0].astype(jnp.int32)
    inv_t, factor, arrived = lax.optimization_barrier((inv_t, factor, arrived))
    for hop in fan_steps:
        inv_t = fan_out(inv_t, hop, grid_pos, grid_size, lambda v, d: v, "grid", 1)
    core_bit = depth_pos % 2
    chip_bit = depth_pos // 2
    cols = jnp.arange(positions - 1, dtype=jnp.int32)
    col_keep = jnp.where(cols % 2 == core_bit, 1 + cols // 2, 3)
    col_send = jnp.where(cols % 2 != core_bit, 1 + cols // 2, 3)
    three = jnp.full((1,), 3, jnp.int32)
    zero = jnp.zeros((1,), jnp.int32)
    keep_of = jnp.concatenate([zero, col_keep, three]).astype(jnp.int32)
    send_of = jnp.concatenate([zero, col_send, three]).astype(jnp.int32)
    keep1, send1 = accumulate(
        arrived_place.reshape(slots), keep_of, send_of, arrived.reshape(slots, tile + 8, tile), 8
    )
    got1 = lax.ppermute(send1, "depth", [(0, 1), (1, 0), (2, 3), (3, 2)])
    sum1 = keep1 + got1
    send2 = jnp.stack([sum1[0], sum1[1 + (1 - chip_bit)]])
    got2 = lax.ppermute(send2, "depth", [(0, 2), (2, 0), (1, 3), (3, 1)])
    panel_sum = sum1[0] + got2[0]
    slab_sum = sum1[1 + chip_bit] + got2[1]

    live = (grid_pos * tile < front_orders[0]).astype(jnp.float32)
    front_panel = (panel_base[0, 0, 0] + panel_sum) * live
    front_slab = (slab_base[0, 0, 0] + slab_sum) * live

    v_here = (grid_pos - depth_pos - 1) % grid_size

    def idx(g, dd):
        return (g % grid_size) * depth_size + dd

    is_a_root = grid_pos == (depth_pos + 1) % grid_size
    pair_a = sum1[0] + panel_base[0, 0, 0]
    payload = jnp.where(is_a_root, pair_a, sum1[0])
    quarters = grid_size // 4
    got0 = []
    for m in range(4):
        perm = []
        for d in range(depth_size):
            if m < 3:
                perm.append((idx(d + 1, d), idx(d + 1 + quarters * (m + 1), d)))
            perm.append((idx(d + 1, d ^ 2), idx(d + 1 + quarters * m, d)))
        got0.append(lax.ppermute(payload, ("grid", "depth"), perm))
    quarter = v_here // quarters
    a_val = pair_a
    b_val = got0[0]
    for m in range(1, 4):
        a_val = jnp.where(quarter == m, got0[m - 1], a_val)
        b_val = jnp.where(quarter == m, got0[m], b_val)
    pair_ab = fan_out(
        jnp.stack([a_val, b_val]), 1, v_here, grid_size,
        lambda v, d: ((v + d + 1) % grid_size) * depth_size + d, ("grid", "depth"), depth_size,
    )
    live_next = ((depth_pos + 1) * tile < front_orders[0]).astype(jnp.float32)
    wanted = (pair_ab[0] + pair_ab[1]) * live_next
    solved = jnp.dot(front_panel, inv_t, precision=HIGH)
    factored = jnp.where(grid_pos == 0, factor, solved)
    wanted = jnp.dot(wanted, inv_t, precision=HIGH)

    update = lax.dot_general(
        factored, wanted, (((1,), (1,)), ((), ())), precision=HIGH
    )
    schur_block = front_slab - update
    return (factored[None, None, None], schur_block[None, None, None])


def solution(mesh):
    in_specs = (
        P("front", None, "grid", None, None),
        P("front", None, "grid", None, "depth"),
        P("front", "grid", "depth", None, None, None),
        P("front", "grid", "depth", None, None),
        P("front"),
    )
    out_specs = (P("front", None, "grid", None, None), P("front", None, "grid", None, "depth"))
    return jax.shard_map(
        on_device, mesh=mesh, in_specs=in_specs, out_specs=out_specs, check_vma=False
    )
```

```python
import jax
import jax.numpy as jnp
from jax import lax
from jax.experimental import pallas as pl
from jax.experimental.pallas import tpu as pltpu
from jax.sharding import PartitionSpec as P

CAP = 2
HIGH = lax.Precision.HIGHEST


def accumulate(place, keep_of, send_of, arrived, chunk):
    slots, rows, tile = arrived.shape

    def kernel(place_ref, keep_ref, send_ref, x_ref, k_out, s_out):
        @pl.when(pl.program_id(0) == 0)
        def _():
            k_out[...] = jnp.zeros_like(k_out)
            s_out[...] = jnp.zeros_like(s_out)

        base = pl.program_id(0) * chunk

        def body(i, carry):
            p = place_ref[base + i]
            x = x_ref[i, pl.ds(0, tile), :]
            k = keep_ref[p]
            kk = jnp.minimum(k, 2)
            k_out[kk] = k_out[kk] + jnp.where(k < 3, x, 0.0)
            j = send_ref[p]
            jj = jnp.minimum(j, 2)
            s_out[jj] = s_out[jj] + jnp.where(j < 3, x, 0.0)
            return carry

        lax.fori_loop(0, chunk, body, 0)

    out = jax.ShapeDtypeStruct((3, tile, tile), jnp.float32)
    return pl.pallas_call(
        kernel,
        grid_spec=pltpu.PrefetchScalarGridSpec(
            num_scalar_prefetch=3,
            grid=(slots // chunk,),
            in_specs=[pl.BlockSpec((chunk, rows, tile), lambda i, a, b, c: (i, 0, 0))],
            out_specs=[
                pl.BlockSpec((3, tile, tile), lambda i, a, b, c: (0, 0, 0)),
                pl.BlockSpec((3, tile, tile), lambda i, a, b, c: (0, 0, 0)),
            ],
        ),
        out_shape=(out, out),
    )(place, keep_of, send_of, arrived)


def route(src, place, tiles, slots):
    kids, tile, _ = tiles.shape

    def kernel(src_ref, place_ref, x_ref, o_ref):
        def body(s, carry):
            k = src_ref[s]
            valid = k < kids
            kk = jnp.minimum(k, kids - 1)
            o_ref[s, pl.ds(0, tile), :] = jnp.where(valid, x_ref[kk], 0.0)
            o_ref[s, pl.ds(tile, 8), :] = jnp.full((8, tile), place_ref[s], jnp.int32).astype(
                jnp.float32
            )
            return carry

        lax.fori_loop(0, slots, body, 0)

    return pl.pallas_call(
        kernel,
        grid_spec=pltpu.PrefetchScalarGridSpec(
            num_scalar_prefetch=2,
            grid=(1,),
            in_specs=[pl.BlockSpec((kids, tile, tile), lambda i, s, p: (0, 0, 0))],
            out_specs=pl.BlockSpec((slots, tile + 8, tile), lambda i, s, p: (0, 0, 0)),
        ),
        out_shape=jax.ShapeDtypeStruct((slots, tile + 8, tile), jnp.float32),
    )(src, place, tiles)


def fan_out(x, hop, v_here, n, index_of, axes, groups):
    out = x
    for m in range(1, 4):
        perm = []
        for d in range(groups):
            for v in range(0, n, 4 * hop):
                if v + m * hop < n:
                    perm.append((index_of(v, d), index_of(v + m * hop, d)))
        got = lax.ppermute(x, axes, perm)
        out = jnp.where(v_here % (4 * hop) == m * hop, got, out)
    return out


def on_device(panel_base, slab_base, child_tiles, child_maps, front_orders):
    grid_size = lax.axis_size("grid")
    depth_size = lax.axis_size("depth")
    grid_pos = lax.axis_index("grid")
    depth_pos = lax.axis_index("depth")
    rounds = panel_base.shape[1]
    tile = panel_base.shape[3]
    column_share = slab_base.shape[4] // tile
    next_tiles = column_share * depth_size
    positions = rounds * (next_tiles + 1)
    assert rounds == 1 and column_share == 1 and depth_size == 4
    assert panel_base.shape[0] == 1 and grid_size == 16
    fan_steps = (grid_size // 4, 1)
    assert grid_size % 4 == 0

    tile_maps = child_maps[0, 0, 0]
    tile_data = child_tiles[0, 0, 0]
    kid_count = tile_data.shape[0]
    parent_row = tile_maps[:, 0]
    parent_col = tile_maps[:, 1]
    owners = parent_row % grid_size
    same_owner = owners[:, None] == owners[None, :]
    earlier = jnp.arange(kid_count)[None, :] < jnp.arange(kid_count)[:, None]
    bucket_slot = jnp.sum((same_owner & earlier).astype(jnp.int32), axis=1)
    destination = owners * CAP + bucket_slot
    slots = grid_size * CAP
    hit = destination[None, :] == jnp.arange(slots)[:, None]
    kid_ids = jnp.arange(kid_count, dtype=jnp.int32)
    src = jnp.sum(jnp.where(hit, kid_ids[None, :], 0), axis=1) + jnp.where(
        jnp.any(hit, axis=1), 0, kid_count
    )
    src = src.astype(jnp.int32)
    position = (parent_row // grid_size * (next_tiles + 1) + parent_col).astype(jnp.int32)
    send_place = jnp.sum(jnp.where(hit, position[None, :], 0), axis=1) + jnp.where(
        jnp.any(hit, axis=1), 0, positions
    )
    send_place = send_place.astype(jnp.int32)
    send_tiles = route(src, send_place, tile_data, slots).reshape(grid_size, CAP, tile + 8, tile)

    factor = jnp.linalg.cholesky(panel_base[0, 0, 0])
    eye = jnp.eye(tile, dtype=jnp.float32)
    inv_t = lax.linalg.triangular_solve(factor, eye, left_side=True, lower=True, transpose_a=True)
    arrived = lax.all_to_all(send_tiles, "grid", 0, 0, tiled=True)
    arrived_place = arrived[:, :, tile, 0].astype(jnp.int32)
    inv_t, factor, arrived = lax.optimization_barrier((inv_t, factor, arrived))
    core_bit = depth_pos % 2
    chip_bit = depth_pos // 2
    cols = jnp.arange(positions - 1, dtype=jnp.int32)
    col_keep = jnp.where(cols % 2 == core_bit, 1 + cols // 2, 3)
    col_send = jnp.where(cols % 2 != core_bit, 1 + cols // 2, 3)
    three = jnp.full((1,), 3, jnp.int32)
    zero = jnp.zeros((1,), jnp.int32)
    keep_of = jnp.concatenate([zero, col_keep, three]).astype(jnp.int32)
    send_of = jnp.concatenate([zero, col_send, three]).astype(jnp.int32)
    got_inv = lax.ppermute(
        inv_t, ("grid", "depth"),
        [(d, ((d + 1) % grid_size) * depth_size + d) for d in range(depth_size)],
    )
    inv_a = jnp.where(grid_pos == (depth_pos + 1) % grid_size, got_inv, inv_t)
    keep1, send1 = accumulate(
        arrived_place.reshape(slots), keep_of, send_of, arrived.reshape(slots, tile + 8, tile), 8
    )
    got1 = lax.ppermute(send1, "depth", [(0, 1), (1, 0), (2, 3), (3, 2)])
    sum1 = keep1 + got1
    send2 = jnp.stack([sum1[0], sum1[1 + (1 - chip_bit)]])
    got2 = lax.ppermute(send2, "depth", [(0, 2), (2, 0), (1, 3), (3, 1)])
    panel_sum = sum1[0] + got2[0]
    slab_sum = sum1[1 + chip_bit] + got2[1]

    live = (grid_pos * tile < front_orders[0]).astype(jnp.float32)
    front_panel = (panel_base[0, 0, 0] + panel_sum) * live
    front_slab = (slab_base[0, 0, 0] + slab_sum) * live

    v_here = (grid_pos - depth_pos - 1) % grid_size

    def idx(g, dd):
        return (g % grid_size) * depth_size + dd

    is_a_root = grid_pos == (depth_pos + 1) % grid_size
    pair_a = sum1[0] + panel_base[0, 0, 0]
    payload = jnp.stack([jnp.where(is_a_root, pair_a, sum1[0]), inv_a])
    quarters = grid_size // 4
    got0 = []
    for m in range(4):
        perm = []
        for d in range(depth_size):
            if m < 3:
                perm.append((idx(d + 1, d), idx(d + 1 + quarters * (m + 1), d)))
            perm.append((idx(d + 1, d ^ 2), idx(d + 1 + quarters * m, d)))
        got0.append(lax.ppermute(payload, ("grid", "depth"), perm))
    quarter = v_here // quarters
    a_val = payload
    b_val = got0[0][0]
    for m in range(1, 4):
        a_val = jnp.where(quarter == m, got0[m - 1], a_val)
        b_val = jnp.where(quarter == m, got0[m][0], b_val)
    pair_ab = fan_out(
        jnp.stack([a_val[0], b_val, a_val[1]]), 1, v_here, grid_size,
        lambda v, d: ((v + d + 1) % grid_size) * depth_size + d, ("grid", "depth"), depth_size,
    )
    inv_t = pair_ab[2]
    live_next = ((depth_pos + 1) * tile < front_orders[0]).astype(jnp.float32)
    wanted = (pair_ab[0] + pair_ab[1]) * live_next
    solved = jnp.dot(front_panel, inv_t, precision=HIGH)
    factored = jnp.where(grid_pos == 0, factor, solved)
    wanted = jnp.dot(wanted, inv_t, precision=HIGH)

    update = lax.dot_general(
        factored, wanted, (((1,), (1,)), ((), ())), precision=HIGH
    )
    schur_block = front_slab - update
    return (factored[None, None, None], schur_block[None, None, None])


def solution(mesh):
    in_specs = (
        P("front", None, "grid", None, None),
        P("front", None, "grid", None, "depth"),
        P("front", "grid", "depth", None, None, None),
        P("front", "grid", "depth", None, None),
        P("front"),
    )
    out_specs = (P("front", None, "grid", None, None), P("front", None, "grid", None, "depth"))
    return jax.shard_map(
        on_device, mesh=mesh, in_specs=in_specs, out_specs=out_specs, check_vma=False
    )
```

```python
import jax
import jax.numpy as jnp
from jax import lax
from jax.experimental import pallas as pl
from jax.experimental.pallas import tpu as pltpu
from jax.sharding import PartitionSpec as P

CAP = 2
HIGH = lax.Precision.HIGHEST


def accumulate(place, keep_of, send_of, arrived, chunk):
    slots, rows, tile = arrived.shape

    def kernel(place_ref, keep_ref, send_ref, x_ref, k_out, s_out):
        @pl.when(pl.program_id(0) == 0)
        def _():
            k_out[...] = jnp.zeros_like(k_out)
            s_out[...] = jnp.zeros_like(s_out)

        base = pl.program_id(0) * chunk

        def body(i, carry):
            p = place_ref[base + i]
            k = keep_ref[p]
            j = send_ref[p]

            @pl.when(k < 3)
            def _():
                k_out[k] = k_out[k] + x_ref[i, pl.ds(0, tile), :]

            @pl.when(j < 3)
            def _():
                s_out[j] = s_out[j] + x_ref[i, pl.ds(0, tile), :]

            return carry

        lax.fori_loop(0, chunk, body, 0)

    out = jax.ShapeDtypeStruct((3, tile, tile), jnp.float32)
    return pl.pallas_call(
        kernel,
        grid_spec=pltpu.PrefetchScalarGridSpec(
            num_scalar_prefetch=3,
            grid=(slots // chunk,),
            in_specs=[pl.BlockSpec((chunk, rows, tile), lambda i, a, b, c: (i, 0, 0))],
            out_specs=[
                pl.BlockSpec((3, tile, tile), lambda i, a, b, c: (0, 0, 0)),
                pl.BlockSpec((3, tile, tile), lambda i, a, b, c: (0, 0, 0)),
            ],
        ),
        out_shape=(out, out),
    )(place, keep_of, send_of, arrived)


def route(src, place, tiles, slots):
    kids, tile, _ = tiles.shape

    def kernel(src_ref, place_ref, x_ref, o_ref):
        def body(s, carry):
            k = src_ref[s]
            valid = k < kids
            kk = jnp.minimum(k, kids - 1)
            o_ref[s, pl.ds(0, tile), :] = jnp.where(valid, x_ref[kk], 0.0)
            o_ref[s, pl.ds(tile, 8), :] = jnp.full((8, tile), place_ref[s], jnp.int32).astype(
                jnp.float32
            )
            return carry

        lax.fori_loop(0, slots, body, 0)

    return pl.pallas_call(
        kernel,
        grid_spec=pltpu.PrefetchScalarGridSpec(
            num_scalar_prefetch=2,
            grid=(1,),
            in_specs=[pl.BlockSpec((kids, tile, tile), lambda i, s, p: (0, 0, 0))],
            out_specs=pl.BlockSpec((slots, tile + 8, tile), lambda i, s, p: (0, 0, 0)),
        ),
        out_shape=jax.ShapeDtypeStruct((slots, tile + 8, tile), jnp.float32),
    )(src, place, tiles)


def fan_out(x, hop, v_here, n, index_of, axes, groups):
    out = x
    for m in range(1, 4):
        perm = []
        for d in range(groups):
            for v in range(0, n, 4 * hop):
                if v + m * hop < n:
                    perm.append((index_of(v, d), index_of(v + m * hop, d)))
        got = lax.ppermute(x, axes, perm)
        out = jnp.where(v_here % (4 * hop) == m * hop, got, out)
    return out


def on_device(panel_base, slab_base, child_tiles, child_maps, front_orders):
    grid_size = lax.axis_size("grid")
    depth_size = lax.axis_size("depth")
    grid_pos = lax.axis_index("grid")
    depth_pos = lax.axis_index("depth")
    rounds = panel_base.shape[1]
    tile = panel_base.shape[3]
    column_share = slab_base.shape[4] // tile
    next_tiles = column_share * depth_size
    positions = rounds * (next_tiles + 1)
    assert rounds == 1 and column_share == 1 and depth_size == 4
    assert panel_base.shape[0] == 1 and grid_size == 16
    fan_steps = (grid_size // 4, 1)

    tile_maps = child_maps[0, 0, 0]
    tile_data = child_tiles[0, 0, 0]
    kid_count = tile_data.shape[0]
    parent_row = tile_maps[:, 0]
    parent_col = tile_maps[:, 1]
    owners = parent_row % grid_size
    same_owner = owners[:, None] == owners[None, :]
    earlier = jnp.arange(kid_count)[None, :] < jnp.arange(kid_count)[:, None]
    bucket_slot = jnp.sum((same_owner & earlier).astype(jnp.int32), axis=1)
    destination = owners * CAP + bucket_slot
    slots = grid_size * CAP
    hit = destination[None, :] == jnp.arange(slots)[:, None]
    kid_ids = jnp.arange(kid_count, dtype=jnp.int32)
    src = jnp.sum(jnp.where(hit, kid_ids[None, :], 0), axis=1) + jnp.where(
        jnp.any(hit, axis=1), 0, kid_count
    )
    src = src.astype(jnp.int32)
    position = (parent_row // grid_size * (next_tiles + 1) + parent_col).astype(jnp.int32)
    send_place = jnp.sum(jnp.where(hit, position[None, :], 0), axis=1) + jnp.where(
        jnp.any(hit, axis=1), 0, positions
    )
    send_place = send_place.astype(jnp.int32)
    send_tiles = route(src, send_place, tile_data, slots).reshape(grid_size, CAP, tile + 8, tile)

    factor = jnp.linalg.cholesky(panel_base[0, 0, 0])
    eye = jnp.eye(tile, dtype=jnp.float32)
    inv_t = lax.linalg.triangular_solve(factor, eye, left_side=True, lower=True, transpose_a=True)
    arrived = lax.all_to_all(send_tiles, "grid", 0, 0, tiled=True)
    arrived_place = arrived[:, :, tile, 0].astype(jnp.int32)
    inv_t, factor, arrived = lax.optimization_barrier((inv_t, factor, arrived))
    for hop in fan_steps:
        inv_t = fan_out(inv_t, hop, grid_pos, grid_size, lambda v, d: v, "grid", 1)
    core_bit = depth_pos % 2
    chip_bit = depth_pos // 2
    cols = jnp.arange(positions - 1, dtype=jnp.int32)
    col_keep = jnp.where(cols % 2 == core_bit, 1 + cols // 2, 3)
    col_send = jnp.where(cols % 2 != core_bit, 1 + cols // 2, 3)
    three = jnp.full((1,), 3, jnp.int32)
    zero = jnp.zeros((1,), jnp.int32)
    keep_of = jnp.concatenate([zero, col_keep, three]).astype(jnp.int32)
    send_of = jnp.concatenate([zero, col_send, three]).astype(jnp.int32)
    keep1, send1 = accumulate(
        arrived_place.reshape(slots), keep_of, send_of, arrived.reshape(slots, tile + 8, tile), 8
    )
    got1 = lax.ppermute(send1, "depth", [(0, 1), (1, 0), (2, 3), (3, 2)])
    sum1 = keep1 + got1
    send2 = jnp.stack([sum1[0], sum1[1 + (1 - chip_bit)]])
    got2 = lax.ppermute(send2, "depth", [(0, 2), (2, 0), (1, 3), (3, 1)])
    panel_sum = sum1[0] + got2[0]
    slab_sum = sum1[1 + chip_bit] + got2[1]

    live = (grid_pos * tile < front_orders[0]).astype(jnp.float32)
    front_panel = (panel_base[0, 0, 0] + panel_sum) * live
    front_slab = (slab_base[0, 0, 0] + slab_sum) * live

    v_here = (grid_pos - depth_pos - 1) % grid_size
    wanted = front_panel
    for hop in fan_steps:
        wanted = fan_out(
            wanted, hop, v_here, grid_size,
            lambda v, d: ((v + d + 1) % grid_size) * depth_size + d, ("grid", "depth"), depth_size,
        )
    solved = jnp.dot(front_panel, inv_t, precision=HIGH)
    factored = jnp.where(grid_pos == 0, factor, solved)
    left = lax.dot_general(factored, inv_t, (((1,), (1,)), ((), ())), precision=HIGH)
    update = lax.dot_general(left, wanted, (((1,), (1,)), ((), ())), precision=HIGH)
    schur_block = front_slab - update
    return (factored[None, None, None], schur_block[None, None, None])


def solution(mesh):
    in_specs = (
        P("front", None, "grid", None, None),
        P("front", None, "grid", None, "depth"),
        P("front", "grid", "depth", None, None, None),
        P("front", "grid", "depth", None, None),
        P("front"),
    )
    out_specs = (P("front", None, "grid", None, None), P("front", None, "grid", None, "depth"))
    return jax.shard_map(
        on_device, mesh=mesh, in_specs=in_specs, out_specs=out_specs, check_vma=False
    )
```

```python
import jax
import jax.numpy as jnp
from jax import lax
from jax.experimental import pallas as pl
from jax.experimental.pallas import tpu as pltpu
from jax.sharding import PartitionSpec as P

CAP = 2
HIGH = lax.Precision.HIGHEST


def accumulate(place, keep_of, send_of, arrived, chunk):
    slots, rows, tile = arrived.shape

    def kernel(place_ref, keep_ref, send_ref, x_ref, k_out, s_out):
        @pl.when(pl.program_id(0) == 0)
        def _():
            k_out[...] = jnp.zeros_like(k_out)
            s_out[...] = jnp.zeros_like(s_out)

        base = pl.program_id(0) * chunk

        def body(i, carry):
            p = place_ref[base + i]
            k = keep_ref[p]
            j = send_ref[p]

            @pl.when(k < 3)
            def _():
                k_out[k] = k_out[k] + x_ref[i, pl.ds(0, tile), :]

            @pl.when(j < 3)
            def _():
                s_out[j] = s_out[j] + x_ref[i, pl.ds(0, tile), :]

            return carry

        lax.fori_loop(0, chunk, body, 0)

    out = jax.ShapeDtypeStruct((3, tile, tile), jnp.float32)
    return pl.pallas_call(
        kernel,
        grid_spec=pltpu.PrefetchScalarGridSpec(
            num_scalar_prefetch=3,
            grid=(slots // chunk,),
            in_specs=[pl.BlockSpec((chunk, rows, tile), lambda i, a, b, c: (i, 0, 0))],
            out_specs=[
                pl.BlockSpec((3, tile, tile), lambda i, a, b, c: (0, 0, 0)),
                pl.BlockSpec((3, tile, tile), lambda i, a, b, c: (0, 0, 0)),
            ],
        ),
        out_shape=(out, out),
    )(place, keep_of, send_of, arrived)


def route(src, place, tiles, slots):
    kids, tile, _ = tiles.shape

    def kernel(src_ref, place_ref, x_ref, o_ref):
        def body(s, carry):
            k = src_ref[s]
            valid = k < kids
            kk = jnp.minimum(k, kids - 1)
            o_ref[s, pl.ds(0, tile), :] = jnp.where(valid, x_ref[kk], 0.0)
            o_ref[s, pl.ds(tile, 8), :] = jnp.full((8, tile), place_ref[s], jnp.int32).astype(
                jnp.float32
            )
            return carry

        lax.fori_loop(0, slots, body, 0)

    return pl.pallas_call(
        kernel,
        grid_spec=pltpu.PrefetchScalarGridSpec(
            num_scalar_prefetch=2,
            grid=(1,),
            in_specs=[pl.BlockSpec((kids, tile, tile), lambda i, s, p: (0, 0, 0))],
            out_specs=pl.BlockSpec((slots, tile + 8, tile), lambda i, s, p: (0, 0, 0)),
        ),
        out_shape=jax.ShapeDtypeStruct((slots, tile + 8, tile), jnp.float32),
    )(src, place, tiles)


def fan_out(x, hop, v_here, n, index_of, axes, groups):
    out = x
    for m in range(1, 4):
        perm = []
        for d in range(groups):
            for v in range(0, n, 4 * hop):
                if v + m * hop < n:
                    perm.append((index_of(v, d), index_of(v + m * hop, d)))
        got = lax.ppermute(x, axes, perm)
        out = jnp.where(v_here % (4 * hop) == m * hop, got, out)
    return out


def on_device(panel_base, slab_base, child_tiles, child_maps, front_orders):
    grid_size = lax.axis_size("grid")
    depth_size = lax.axis_size("depth")
    grid_pos = lax.axis_index("grid")
    depth_pos = lax.axis_index("depth")
    rounds = panel_base.shape[1]
    tile = panel_base.shape[3]
    column_share = slab_base.shape[4] // tile
    next_tiles = column_share * depth_size
    positions = rounds * (next_tiles + 1)
    assert rounds == 1 and column_share == 1 and depth_size == 4
    assert panel_base.shape[0] == 1 and grid_size == 16
    fan_steps = (grid_size // 4, 1)

    tile_maps = child_maps[0, 0, 0]
    tile_data = child_tiles[0, 0, 0]
    kid_count = tile_data.shape[0]
    parent_row = tile_maps[:, 0]
    parent_col = tile_maps[:, 1]
    owners = parent_row % grid_size
    same_owner = owners[:, None] == owners[None, :]
    earlier = jnp.arange(kid_count)[None, :] < jnp.arange(kid_count)[:, None]
    bucket_slot = jnp.sum((same_owner & earlier).astype(jnp.int32), axis=1)
    destination = owners * CAP + bucket_slot
    slots = grid_size * CAP
    hit = destination[None, :] == jnp.arange(slots)[:, None]
    kid_ids = jnp.arange(kid_count, dtype=jnp.int32)
    src = jnp.sum(jnp.where(hit, kid_ids[None, :], 0), axis=1) + jnp.where(
        jnp.any(hit, axis=1), 0, kid_count
    )
    src = src.astype(jnp.int32)
    position = (parent_row // grid_size * (next_tiles + 1) + parent_col).astype(jnp.int32)
    send_place = jnp.sum(jnp.where(hit, position[None, :], 0), axis=1) + jnp.where(
        jnp.any(hit, axis=1), 0, positions
    )
    send_place = send_place.astype(jnp.int32)
    send_tiles = route(src, send_place, tile_data, slots).reshape(grid_size, CAP, tile + 8, tile)

    factor = jnp.linalg.cholesky(panel_base[0, 0, 0])
    eye = jnp.eye(tile, dtype=jnp.float32)
    inv_t = lax.linalg.triangular_solve(factor, eye, left_side=True, lower=True, transpose_a=True)
    arrived = lax.all_to_all(send_tiles, "grid", 0, 0, tiled=True)
    arrived_place = arrived[:, :, tile, 0].astype(jnp.int32)
    inv_all = inv_t
    for k in range(1, grid_size):
        got = lax.ppermute(inv_t, "grid", [(0, k)])
        inv_all = jnp.where(grid_pos == k, got, inv_all)
    inv_t, factor, arrived = lax.optimization_barrier((inv_all, factor, arrived))
    core_bit = depth_pos % 2
    chip_bit = depth_pos // 2
    cols = jnp.arange(positions - 1, dtype=jnp.int32)
    col_keep = jnp.where(cols % 2 == core_bit, 1 + cols // 2, 3)
    col_send = jnp.where(cols % 2 != core_bit, 1 + cols // 2, 3)
    three = jnp.full((1,), 3, jnp.int32)
    zero = jnp.zeros((1,), jnp.int32)
    keep_of = jnp.concatenate([zero, col_keep, three]).astype(jnp.int32)
    send_of = jnp.concatenate([zero, col_send, three]).astype(jnp.int32)
    keep1, send1 = accumulate(
        arrived_place.reshape(slots), keep_of, send_of, arrived.reshape(slots, tile + 8, tile), 8
    )
    got1 = lax.ppermute(send1, "depth", [(0, 1), (1, 0), (2, 3), (3, 2)])
    sum1 = keep1 + got1
    send2 = jnp.stack([sum1[0], sum1[1 + (1 - chip_bit)]])
    got2 = lax.ppermute(send2, "depth", [(0, 2), (2, 0), (1, 3), (3, 1)])
    panel_sum = sum1[0] + got2[0]
    slab_sum = sum1[1 + chip_bit] + got2[1]

    live = (grid_pos * tile < front_orders[0]).astype(jnp.float32)
    front_panel = (panel_base[0, 0, 0] + panel_sum) * live
    front_slab = (slab_base[0, 0, 0] + slab_sum) * live

    v_here = (grid_pos - depth_pos - 1) % grid_size
    wanted = front_panel
    for hop in fan_steps:
        wanted = fan_out(
            wanted, hop, v_here, grid_size,
            lambda v, d: ((v + d + 1) % grid_size) * depth_size + d, ("grid", "depth"), depth_size,
        )
    solved = jnp.dot(front_panel, inv_t, precision=HIGH)
    factored = jnp.where(grid_pos == 0, factor, solved)
    left = lax.dot_general(factored, inv_t, (((1,), (1,)), ((), ())), precision=HIGH)
    update = lax.dot_general(left, wanted, (((1,), (1,)), ((), ())), precision=HIGH)
    schur_block = front_slab - update
    return (factored[None, None, None], schur_block[None, None, None])


def solution(mesh):
    in_specs = (
        P("front", None, "grid", None, None),
        P("front", None, "grid", None, "depth"),
        P("front", "grid", "depth", None, None, None),
        P("front", "grid", "depth", None, None),
        P("front"),
    )
    out_specs = (P("front", None, "grid", None, None), P("front", None, "grid", None, "depth"))
    return jax.shard_map(
        on_device, mesh=mesh, in_specs=in_specs, out_specs=out_specs, check_vma=False
    )
```

```python
import jax
import jax.numpy as jnp
from jax import lax
from jax.experimental import pallas as pl
from jax.experimental.pallas import tpu as pltpu
from jax.sharding import PartitionSpec as P

CAP = 2
HIGH = lax.Precision.HIGHEST


def accumulate(place, keep_of, send_of, arrived, chunk):
    slots, rows, tile = arrived.shape

    def kernel(place_ref, keep_ref, send_ref, x_ref, k_out, s_out):
        @pl.when(pl.program_id(0) == 0)
        def _():
            k_out[...] = jnp.zeros_like(k_out)
            s_out[...] = jnp.zeros_like(s_out)

        base = pl.program_id(0) * chunk

        def body(i, carry):
            p = place_ref[base + i]
            k = keep_ref[p]
            j = send_ref[p]

            @pl.when(k < 3)
            def _():
                k_out[k] = k_out[k] + x_ref[i, pl.ds(0, tile), :]

            @pl.when(j < 3)
            def _():
                s_out[j] = s_out[j] + x_ref[i, pl.ds(0, tile), :]

            return carry

        lax.fori_loop(0, chunk, body, 0)

    out = jax.ShapeDtypeStruct((3, tile, tile), jnp.float32)
    return pl.pallas_call(
        kernel,
        grid_spec=pltpu.PrefetchScalarGridSpec(
            num_scalar_prefetch=3,
            grid=(slots // chunk,),
            in_specs=[pl.BlockSpec((chunk, rows, tile), lambda i, a, b, c: (i, 0, 0))],
            out_specs=[
                pl.BlockSpec((3, tile, tile), lambda i, a, b, c: (0, 0, 0)),
                pl.BlockSpec((3, tile, tile), lambda i, a, b, c: (0, 0, 0)),
            ],
        ),
        out_shape=(out, out),
    )(place, keep_of, send_of, arrived)


def route(src, place, tiles, slots, chunk=8):
    kids, tile, _ = tiles.shape

    def kernel(src_ref, place_ref, x_ref, o_ref):
        base = pl.program_id(0) * chunk

        def body(i, carry):
            k = src_ref[base + i]
            valid = k < kids
            kk = jnp.minimum(k, kids - 1)
            o_ref[i, pl.ds(0, tile), :] = jnp.where(valid, x_ref[kk], 0.0)
            o_ref[i, pl.ds(tile, 8), :] = jnp.full(
                (8, tile), place_ref[base + i], jnp.int32
            ).astype(jnp.float32)
            return carry

        lax.fori_loop(0, chunk, body, 0)

    return pl.pallas_call(
        kernel,
        grid_spec=pltpu.PrefetchScalarGridSpec(
            num_scalar_prefetch=2,
            grid=(slots // chunk,),
            in_specs=[pl.BlockSpec((kids, tile, tile), lambda i, s, p: (0, 0, 0))],
            out_specs=pl.BlockSpec((chunk, tile + 8, tile), lambda i, s, p: (i, 0, 0)),
        ),
        out_shape=jax.ShapeDtypeStruct((slots, tile + 8, tile), jnp.float32),
    )(src, place, tiles)


def fan_out(x, hop, v_here, n, index_of, axes, groups):
    out = x
    for m in range(1, 4):
        perm = []
        for d in range(groups):
            for v in range(0, n, 4 * hop):
                if v + m * hop < n:
                    perm.append((index_of(v, d), index_of(v + m * hop, d)))
        got = lax.ppermute(x, axes, perm)
        out = jnp.where(v_here % (4 * hop) == m * hop, got, out)
    return out


def on_device(panel_base, slab_base, child_tiles, child_maps, front_orders):
    grid_size = lax.axis_size("grid")
    depth_size = lax.axis_size("depth")
    grid_pos = lax.axis_index("grid")
    depth_pos = lax.axis_index("depth")
    rounds = panel_base.shape[1]
    tile = panel_base.shape[3]
    column_share = slab_base.shape[4] // tile
    next_tiles = column_share * depth_size
    positions = rounds * (next_tiles + 1)
    assert rounds == 1 and column_share == 1 and depth_size == 4
    assert panel_base.shape[0] == 1 and grid_size == 16
    fan_steps = (grid_size // 4, 1)

    tile_maps = child_maps[0, 0, 0]
    tile_data = child_tiles[0, 0, 0]
    kid_count = tile_data.shape[0]
    parent_row = tile_maps[:, 0]
    parent_col = tile_maps[:, 1]
    owners = parent_row % grid_size
    same_owner = owners[:, None] == owners[None, :]
    earlier = jnp.arange(kid_count)[None, :] < jnp.arange(kid_count)[:, None]
    bucket_slot = jnp.sum((same_owner & earlier).astype(jnp.int32), axis=1)
    destination = owners * CAP + bucket_slot
    slots = grid_size * CAP
    hit = destination[None, :] == jnp.arange(slots)[:, None]
    kid_ids = jnp.arange(kid_count, dtype=jnp.int32)
    src = jnp.sum(jnp.where(hit, kid_ids[None, :], 0), axis=1) + jnp.where(
        jnp.any(hit, axis=1), 0, kid_count
    )
    src = src.astype(jnp.int32)
    position = (parent_row // grid_size * (next_tiles + 1) + parent_col).astype(jnp.int32)
    send_place = jnp.sum(jnp.where(hit, position[None, :], 0), axis=1) + jnp.where(
        jnp.any(hit, axis=1), 0, positions
    )
    send_place = send_place.astype(jnp.int32)
    send_tiles = route(src, send_place, tile_data, slots).reshape(grid_size, CAP, tile + 8, tile)

    factor = jnp.linalg.cholesky(panel_base[0, 0, 0])
    eye = jnp.eye(tile, dtype=jnp.float32)
    inv_t = lax.linalg.triangular_solve(factor, eye, left_side=True, lower=True, transpose_a=True)
    arrived = lax.all_to_all(send_tiles, "grid", 0, 0, tiled=True)
    arrived_place = arrived[:, :, tile, 0].astype(jnp.int32)
    inv_t, factor, arrived = lax.optimization_barrier((inv_t, factor, arrived))
    for hop in fan_steps:
        inv_t = fan_out(inv_t, hop, grid_pos, grid_size, lambda v, d: v, "grid", 1)
    core_bit = depth_pos % 2
    chip_bit = depth_pos // 2
    cols = jnp.arange(positions - 1, dtype=jnp.int32)
    col_keep = jnp.where(cols % 2 == core_bit, 1 + cols // 2, 3)
    col_send = jnp.where(cols % 2 != core_bit, 1 + cols // 2, 3)
    three = jnp.full((1,), 3, jnp.int32)
    zero = jnp.zeros((1,), jnp.int32)
    keep_of = jnp.concatenate([zero, col_keep, three]).astype(jnp.int32)
    send_of = jnp.concatenate([zero, col_send, three]).astype(jnp.int32)
    keep1, send1 = accumulate(
        arrived_place.reshape(slots), keep_of, send_of, arrived.reshape(slots, tile + 8, tile), 8
    )
    got1 = lax.ppermute(send1, "depth", [(0, 1), (1, 0), (2, 3), (3, 2)])
    sum1 = keep1 + got1
    send2 = jnp.stack([sum1[0], sum1[1 + (1 - chip_bit)]])
    got2 = lax.ppermute(send2, "depth", [(0, 2), (2, 0), (1, 3), (3, 1)])
    panel_sum = sum1[0] + got2[0]
    slab_sum = sum1[1 + chip_bit] + got2[1]

    live = (grid_pos * tile < front_orders[0]).astype(jnp.float32)
    front_panel = (panel_base[0, 0, 0] + panel_sum) * live
    front_slab = (slab_base[0, 0, 0] + slab_sum) * live

    v_here = (grid_pos - depth_pos - 1) % grid_size
    wanted = front_panel
    for hop in fan_steps:
        wanted = fan_out(
            wanted, hop, v_here, grid_size,
            lambda v, d: ((v + d + 1) % grid_size) * depth_size + d, ("grid", "depth"), depth_size,
        )
    solved = jnp.dot(front_panel, inv_t, precision=HIGH)
    factored = jnp.where(grid_pos == 0, factor, solved)
    left = lax.dot_general(factored, inv_t, (((1,), (1,)), ((), ())), precision=HIGH)
    update = lax.dot_general(left, wanted, (((1,), (1,)), ((), ())), precision=HIGH)
    schur_block = front_slab - update
    return (factored[None, None, None], schur_block[None, None, None])


def solution(mesh):
    in_specs = (
        P("front", None, "grid", None, None),
        P("front", None, "grid", None, "depth"),
        P("front", "grid", "depth", None, None, None),
        P("front", "grid", "depth", None, None),
        P("front"),
    )
    out_specs = (P("front", None, "grid", None, None), P("front", None, "grid", None, "depth"))
    return jax.shard_map(
        on_device, mesh=mesh, in_specs=in_specs, out_specs=out_specs, check_vma=False
    )
```

```python
import jax
import jax.numpy as jnp
from jax import lax
from jax.experimental import pallas as pl
from jax.experimental.pallas import tpu as pltpu
from jax.sharding import PartitionSpec as P

CAP = 2
HIGH = lax.Precision.HIGHEST


def accumulate(place, keep_of, send_of, arrived, chunk):
    slots, rows, tile = arrived.shape

    def kernel(place_ref, keep_ref, send_ref, x_ref, k_out, s_out):
        @pl.when(pl.program_id(0) == 0)
        def _():
            k_out[...] = jnp.zeros_like(k_out)
            s_out[...] = jnp.zeros_like(s_out)

        base = pl.program_id(0) * chunk

        def body(i, carry):
            p = place_ref[base + i]
            x = x_ref[i, pl.ds(0, tile), :]
            k = keep_ref[p]
            kk = jnp.minimum(k, 2)
            k_out[kk] = k_out[kk] + jnp.where(k < 3, x, 0.0)
            j = send_ref[p]
            jj = jnp.minimum(j, 2)
            s_out[jj] = s_out[jj] + jnp.where(j < 3, x, 0.0)
            return carry

        lax.fori_loop(0, chunk, body, 0)

    out = jax.ShapeDtypeStruct((3, tile, tile), jnp.float32)
    return pl.pallas_call(
        kernel,
        grid_spec=pltpu.PrefetchScalarGridSpec(
            num_scalar_prefetch=3,
            grid=(slots // chunk,),
            in_specs=[pl.BlockSpec((chunk, rows, tile), lambda i, a, b, c: (i, 0, 0))],
            out_specs=[
                pl.BlockSpec((3, tile, tile), lambda i, a, b, c: (0, 0, 0)),
                pl.BlockSpec((3, tile, tile), lambda i, a, b, c: (0, 0, 0)),
            ],
        ),
        out_shape=(out, out),
    )(place, keep_of, send_of, arrived)


def route(src, place, tiles, slots):
    kids, tile, _ = tiles.shape

    def kernel(src_ref, place_ref, x_ref, o_ref):
        def body(s, carry):
            k = src_ref[s]
            valid = k < kids
            kk = jnp.minimum(k, kids - 1)
            o_ref[s, pl.ds(0, tile), :] = jnp.where(valid, x_ref[kk], 0.0)
            o_ref[s, pl.ds(tile, 8), :] = jnp.full((8, tile), place_ref[s], jnp.int32).astype(
                jnp.float32
            )
            return carry

        lax.fori_loop(0, slots, body, 0)

    return pl.pallas_call(
        kernel,
        grid_spec=pltpu.PrefetchScalarGridSpec(
            num_scalar_prefetch=2,
            grid=(1,),
            in_specs=[pl.BlockSpec((kids, tile, tile), lambda i, s, p: (0, 0, 0))],
            out_specs=pl.BlockSpec((slots, tile + 8, tile), lambda i, s, p: (0, 0, 0)),
        ),
        out_shape=jax.ShapeDtypeStruct((slots, tile + 8, tile), jnp.float32),
    )(src, place, tiles)


def fan_out(x, hop, v_here, n, index_of, axes, groups):
    out = x
    for m in range(1, 4):
        perm = []
        for d in range(groups):
            for v in range(0, n, 4 * hop):
                if v + m * hop < n:
                    perm.append((index_of(v, d), index_of(v + m * hop, d)))
        got = lax.ppermute(x, axes, perm)
        out = jnp.where(v_here % (4 * hop) == m * hop, got, out)
    return out


def on_device(panel_base, slab_base, child_tiles, child_maps, front_orders):
    grid_size = lax.axis_size("grid")
    depth_size = lax.axis_size("depth")
    grid_pos = lax.axis_index("grid")
    depth_pos = lax.axis_index("depth")
    rounds = panel_base.shape[1]
    tile = panel_base.shape[3]
    column_share = slab_base.shape[4] // tile
    next_tiles = column_share * depth_size
    positions = rounds * (next_tiles + 1)
    assert rounds == 1 and column_share == 1 and depth_size == 4
    assert panel_base.shape[0] == 1 and grid_size == 16
    fan_steps = (grid_size // 4, 1)

    tile_maps = child_maps[0, 0, 0]
    tile_data = child_tiles[0, 0, 0]
    kid_count = tile_data.shape[0]
    parent_row = tile_maps[:, 0]
    parent_col = tile_maps[:, 1]
    owners = parent_row % grid_size
    same_owner = owners[:, None] == owners[None, :]
    earlier = jnp.arange(kid_count)[None, :] < jnp.arange(kid_count)[:, None]
    bucket_slot = jnp.sum((same_owner & earlier).astype(jnp.int32), axis=1)
    destination = owners * CAP + bucket_slot
    slots = grid_size * CAP
    hit = destination[None, :] == jnp.arange(slots)[:, None]
    kid_ids = jnp.arange(kid_count, dtype=jnp.int32)
    src = jnp.sum(jnp.where(hit, kid_ids[None, :], 0), axis=1) + jnp.where(
        jnp.any(hit, axis=1), 0, kid_count
    )
    src = src.astype(jnp.int32)
    position = (parent_row // grid_size * (next_tiles + 1) + parent_col).astype(jnp.int32)
    send_place = jnp.sum(jnp.where(hit, position[None, :], 0), axis=1) + jnp.where(
        jnp.any(hit, axis=1), 0, positions
    )
    send_place = send_place.astype(jnp.int32)
    send_tiles = route(src, send_place, tile_data, slots).reshape(grid_size, CAP, tile + 8, tile)

    factor = jnp.linalg.cholesky(panel_base[0, 0, 0])
    eye = jnp.eye(tile, dtype=jnp.float32)
    inv_t = lax.linalg.triangular_solve(factor, eye, left_side=True, lower=True, transpose_a=True)
    arrived = lax.all_to_all(send_tiles, "grid", 0, 0, tiled=True)
    arrived_place = arrived[:, :, tile, 0].astype(jnp.int32)
    inv_t, factor, arrived = lax.optimization_barrier((inv_t, factor, arrived))
    core_bit = depth_pos % 2
    chip_bit = depth_pos // 2
    cols = jnp.arange(positions - 1, dtype=jnp.int32)
    col_keep = jnp.where(cols % 2 == core_bit, 1 + cols // 2, 3)
    col_send = jnp.where(cols % 2 != core_bit, 1 + cols // 2, 3)
    three = jnp.full((1,), 3, jnp.int32)
    zero = jnp.zeros((1,), jnp.int32)
    keep_of = jnp.concatenate([zero, col_keep, three]).astype(jnp.int32)
    send_of = jnp.concatenate([zero, col_send, three]).astype(jnp.int32)
    keep1, send1 = accumulate(
        arrived_place.reshape(slots), keep_of, send_of, arrived.reshape(slots, tile + 8, tile), 8
    )
    got1 = lax.ppermute(send1, "depth", [(0, 1), (1, 0), (2, 3), (3, 2)])
    sum1 = keep1 + got1
    inv_t, sum1 = lax.optimization_barrier((inv_t, sum1))
    for hop in fan_steps:
        inv_t = fan_out(inv_t, hop, grid_pos, grid_size, lambda v, d: v, "grid", 1)
    send2 = jnp.stack([sum1[0], sum1[1 + (1 - chip_bit)]])
    got2 = lax.ppermute(send2, "depth", [(0, 2), (2, 0), (1, 3), (3, 1)])
    panel_sum = sum1[0] + got2[0]
    slab_sum = sum1[1 + chip_bit] + got2[1]

    live = (grid_pos * tile < front_orders[0]).astype(jnp.float32)
    front_panel = (panel_base[0, 0, 0] + panel_sum) * live
    front_slab = (slab_base[0, 0, 0] + slab_sum) * live

    v_here = (grid_pos - depth_pos - 1) % grid_size
    wanted = front_panel
    for hop in fan_steps:
        wanted = fan_out(
            wanted, hop, v_here, grid_size,
            lambda v, d: ((v + d + 1) % grid_size) * depth_size + d, ("grid", "depth"), depth_size,
        )
    solved = jnp.dot(front_panel, inv_t, precision=HIGH)
    factored = jnp.where(grid_pos == 0, factor, solved)
    wanted = jnp.dot(wanted, inv_t, precision=HIGH)

    update = lax.dot_general(
        factored, wanted, (((1,), (1,)), ((), ())), precision=HIGH
    )
    schur_block = front_slab - update
    return (factored[None, None, None], schur_block[None, None, None])


def solution(mesh):
    in_specs = (
        P("front", None, "grid", None, None),
        P("front", None, "grid", None, "depth"),
        P("front", "grid", "depth", None, None, None),
        P("front", "grid", "depth", None, None),
        P("front"),
    )
    out_specs = (P("front", None, "grid", None, None), P("front", None, "grid", None, "depth"))
    return jax.shard_map(
        on_device, mesh=mesh, in_specs=in_specs, out_specs=out_specs, check_vma=False
    )
```

```python
import jax
import jax.numpy as jnp
from jax import lax
from jax.experimental import pallas as pl
from jax.experimental.pallas import tpu as pltpu
from jax.sharding import PartitionSpec as P

CAP = 2
HIGH = lax.Precision.HIGHEST


def accumulate(place, keep_of, send_of, arrived, chunk):
    slots, rows, tile = arrived.shape

    def kernel(place_ref, keep_ref, send_ref, x_ref, k_out, s_out):
        @pl.when(pl.program_id(0) == 0)
        def _():
            k_out[...] = jnp.zeros_like(k_out)
            s_out[...] = jnp.zeros_like(s_out)

        base = pl.program_id(0) * chunk

        def body(i, carry):
            p = place_ref[base + i]
            x = x_ref[i, pl.ds(0, tile), :]
            k = keep_ref[p]
            kk = jnp.minimum(k, 2)
            k_out[kk] = k_out[kk] + jnp.where(k < 3, x, 0.0)
            j = send_ref[p]
            jj = jnp.minimum(j, 2)
            s_out[jj] = s_out[jj] + jnp.where(j < 3, x, 0.0)
            return carry

        lax.fori_loop(0, chunk, body, 0)

    out = jax.ShapeDtypeStruct((3, tile, tile), jnp.float32)
    return pl.pallas_call(
        kernel,
        grid_spec=pltpu.PrefetchScalarGridSpec(
            num_scalar_prefetch=3,
            grid=(slots // chunk,),
            in_specs=[pl.BlockSpec((chunk, rows, tile), lambda i, a, b, c: (i, 0, 0))],
            out_specs=[
                pl.BlockSpec((3, tile, tile), lambda i, a, b, c: (0, 0, 0)),
                pl.BlockSpec((3, tile, tile), lambda i, a, b, c: (0, 0, 0)),
            ],
        ),
        out_shape=(out, out),
    )(place, keep_of, send_of, arrived)


def route(src, place, tiles, slots):
    kids, tile, _ = tiles.shape

    def kernel(src_ref, place_ref, x_ref, o_ref):
        def body(s, carry):
            k = src_ref[s]
            valid = k < kids
            kk = jnp.minimum(k, kids - 1)
            o_ref[s, pl.ds(0, tile), :] = jnp.where(valid, x_ref[kk], 0.0)
            o_ref[s, pl.ds(tile, 8), :] = jnp.full((8, tile), place_ref[s], jnp.int32).astype(
                jnp.float32
            )
            return carry

        lax.fori_loop(0, slots, body, 0)

    return pl.pallas_call(
        kernel,
        grid_spec=pltpu.PrefetchScalarGridSpec(
            num_scalar_prefetch=2,
            grid=(1,),
            in_specs=[pl.BlockSpec((kids, tile, tile), lambda i, s, p: (0, 0, 0))],
            out_specs=pl.BlockSpec((slots, tile + 8, tile), lambda i, s, p: (0, 0, 0)),
        ),
        out_shape=jax.ShapeDtypeStruct((slots, tile + 8, tile), jnp.float32),
    )(src, place, tiles)


def fan_out(x, hop, v_here, n, index_of, axes, groups):
    out = x
    for m in range(1, 4):
        perm = []
        for d in range(groups):
            for v in range(0, n, 4 * hop):
                if v + m * hop < n:
                    perm.append((index_of(v, d), index_of(v + m * hop, d)))
        got = lax.ppermute(x, axes, perm)
        out = jnp.where(v_here % (4 * hop) == m * hop, got, out)
    return out


def on_device(panel_base, slab_base, child_tiles, child_maps, front_orders):
    grid_size = lax.axis_size("grid")
    depth_size = lax.axis_size("depth")
    grid_pos = lax.axis_index("grid")
    depth_pos = lax.axis_index("depth")
    rounds = panel_base.shape[1]
    tile = panel_base.shape[3]
    column_share = slab_base.shape[4] // tile
    next_tiles = column_share * depth_size
    positions = rounds * (next_tiles + 1)
    assert rounds == 1 and column_share == 1 and depth_size == 4
    assert panel_base.shape[0] == 1 and grid_size == 16
    fan_steps = (grid_size // 4, 1)

    tile_maps = child_maps[0, 0, 0]
    tile_data = child_tiles[0, 0, 0]
    kid_count = tile_data.shape[0]
    parent_row = tile_maps[:, 0]
    parent_col = tile_maps[:, 1]
    owners = parent_row % grid_size
    same_owner = owners[:, None] == owners[None, :]
    earlier = jnp.arange(kid_count)[None, :] < jnp.arange(kid_count)[:, None]
    bucket_slot = jnp.sum((same_owner & earlier).astype(jnp.int32), axis=1)
    destination = owners * CAP + bucket_slot
    slots = grid_size * CAP
    hit = destination[None, :] == jnp.arange(slots)[:, None]
    kid_ids = jnp.arange(kid_count, dtype=jnp.int32)
    src = jnp.sum(jnp.where(hit, kid_ids[None, :], 0), axis=1) + jnp.where(
        jnp.any(hit, axis=1), 0, kid_count
    )
    src = src.astype(jnp.int32)
    position = (parent_row // grid_size * (next_tiles + 1) + parent_col).astype(jnp.int32)
    send_place = jnp.sum(jnp.where(hit, position[None, :], 0), axis=1) + jnp.where(
        jnp.any(hit, axis=1), 0, positions
    )
    send_place = send_place.astype(jnp.int32)
    send_tiles = route(src, send_place, tile_data, slots).reshape(grid_size, CAP, tile + 8, tile)

    factor = jnp.linalg.cholesky(panel_base[0, 0, 0])
    eye = jnp.eye(tile, dtype=jnp.float32)
    inv_t = lax.linalg.triangular_solve(factor, eye, left_side=True, lower=True, transpose_a=True)
    arrived = lax.all_to_all(send_tiles, "grid", 0, 0, tiled=True)
    arrived_place = arrived[:, :, tile, 0].astype(jnp.int32)
    inv_t, factor, arrived = lax.optimization_barrier((inv_t, factor, arrived))
    for hop in fan_steps:
        inv_t = fan_out(inv_t, hop, grid_pos, grid_size, lambda v, d: v, "grid", 1)
    core_bit = depth_pos % 2
    chip_bit = depth_pos // 2
    cols = jnp.arange(positions - 1, dtype=jnp.int32)
    col_keep = jnp.where(cols % 2 == core_bit, 1 + cols // 2, 3)
    col_send = jnp.where(cols % 2 != core_bit, 1 + cols // 2, 3)
    three = jnp.full((1,), 3, jnp.int32)
    zero = jnp.zeros((1,), jnp.int32)
    keep_of = jnp.concatenate([zero, col_keep, three]).astype(jnp.int32)
    send_of = jnp.concatenate([zero, col_send, three]).astype(jnp.int32)
    keep1, send1 = accumulate(
        arrived_place.reshape(slots), keep_of, send_of, arrived.reshape(slots, tile + 8, tile), slots
    )
    got1 = lax.ppermute(send1, "depth", [(0, 1), (1, 0), (2, 3), (3, 2)])
    sum1 = keep1 + got1
    send2 = jnp.stack([sum1[0], sum1[1 + (1 - chip_bit)]])
    got2 = lax.ppermute(send2, "depth", [(0, 2), (2, 0), (1, 3), (3, 1)])
    panel_sum = sum1[0] + got2[0]
    slab_sum = sum1[1 + chip_bit] + got2[1]

    live = (grid_pos * tile < front_orders[0]).astype(jnp.float32)
    front_panel = (panel_base[0, 0, 0] + panel_sum) * live
    front_slab = (slab_base[0, 0, 0] + slab_sum) * live

    v_here = (grid_pos - depth_pos - 1) % grid_size
    wanted = front_panel
    for hop in fan_steps:
        wanted = fan_out(
            wanted, hop, v_here, grid_size,
            lambda v, d: ((v + d + 1) % grid_size) * depth_size + d, ("grid", "depth"), depth_size,
        )
    solved = jnp.dot(front_panel, inv_t, precision=HIGH)
    factored = jnp.where(grid_pos == 0, factor, solved)
    wanted = jnp.dot(wanted, inv_t, precision=HIGH)

    update = lax.dot_general(
        factored, wanted, (((1,), (1,)), ((), ())), precision=HIGH
    )
    schur_block = front_slab - update
    return (factored[None, None, None], schur_block[None, None, None])


def solution(mesh):
    in_specs = (
        P("front", None, "grid", None, None),
        P("front", None, "grid", None, "depth"),
        P("front", "grid", "depth", None, None, None),
        P("front", "grid", "depth", None, None),
        P("front"),
    )
    out_specs = (P("front", None, "grid", None, None), P("front", None, "grid", None, "depth"))
    return jax.shard_map(
        on_device, mesh=mesh, in_specs=in_specs, out_specs=out_specs, check_vma=False
    )
```
